32 devices in a mesh: group: 2 (over y), dp: 4 (over x, core), section: 4 (over z).
Axes of the slice: x: 2, y: 2, z: 4, core: 2. Of those that a mesh axis runs over, the one named last changes fastest.
Arguments:
- features: bfloat16 [32, 16, 16, 384], P(('group', 'dp')), parts along dimension 0, may hold values from -16 to 16
- init_noise: float32 [32, 16, 16, 384], P(('group', 'dp')), parts along dimension 0, may hold values from -0.5 to 0.5
- target: bfloat16 [32, 16, 16, 384], P(('group', 'dp')), parts along dimension 0, may hold values from -6 to 6
- kernel: float32 [4, 384, 49], P('section'), may hold values from -0.875 to 0.875
- norm_gain: float32 [4, 384], P('section'), may hold values from 0.1 to 1.9
- layer_scale: float32 [4, 384], P('section'), may hold values from 0.2 to 1
- w_in: bfloat16 [4, 384, 1536], P('section', 'dp'), may hold values from -0.3125 to 0.3125
- w_out: bfloat16 [4, 1536, 384], P('section', 'dp'), may hold values from -0.15625 to 0.15625
Outputs:
- grad_kernel: float32 [8, 384, 49], P(('group', 'section'), 'dp'), parts along dimension 0
- grad_w_in: float32 [8, 384, 1536], P(('group', 'section'), 'dp'), parts along dimension 0
- grad_w_out: float32 [8, 1536, 384], P(('group', 'section'), 'dp'), parts along dimension 0
The draws below stay inside these ranges and needn't reach their ends.
There are 2 independent parts, one for each index of `group`. The reference program is written for one: setup_inputs(seed, part) draws one part's arguments, and reference() takes and returns one part's arrays. A program takes and returns all parts, laid end to end along the dimension named above; an argument that names none is the same for every part. Nothing has to cross between parts.
All inputs are finite; a program needn't handle non-finite values.
Results may differ from the reference program's by a relative error of at most 0.012.
Values may be sent and summed in bfloat16 or wider, within the bound.
No kernel may reach another device: no remote copies, remote signals or barrier semaphores. Data moves between devices by JAX's collectives and lax.ppermute only.
A program may use at most 192 MiB of HBM per device.

```python
import math
import jax
import jax.numpy as jnp
from jax import lax

C = 384
HID = 1536
KK = 49
SIDE = 16
IMAGES = 16
BLOCKS = 4
TOKENS = 4096


def draw_features(key, part):
    subkeys = jax.random.split(key, 3)
    low_end = math.log(0.5)
    high_end = math.log(2.0)
    row_scale = jnp.exp(jax.random.uniform(subkeys[0], (IMAGES, SIDE, SIDE, 1), jnp.float32, low_end, high_end))
    col_scale = jnp.exp(jax.random.uniform(subkeys[1], (1, 1, 1, C), jnp.float32, low_end, high_end))
    base_draw = jnp.clip(jax.random.normal(subkeys[2], (IMAGES, SIDE, SIDE, C), jnp.float32), -4.0, 4.0)
    return (base_draw * row_scale * col_scale).astype(jnp.bfloat16)


def steps_of(key, dims, cuts, least, top_value):
    level, own = 1.0, jax.random.fold_in(key, 6)
    for position, shards_of in cuts:
        heights = jnp.exp(jax.random.uniform(jax.random.fold_in(own, position), (shards_of,), jnp.float32, least / len(cuts), top_value / len(cuts)))
        level = level * jnp.repeat(heights, dims[position] // shards_of).reshape([-1 if axis == position else 1 for axis in range(len(dims))])
    return level


def bell_draw(rng, shape, deviation, limit, cuts=(), held_as=jnp.bfloat16):
    array = jax.random.normal(rng, shape, jnp.float32) * deviation
    if len(cuts) > 0:
        array = steps_of(rng, shape, cuts, -0.22, 0.18) * array
    return jnp.clip(array, min=-limit, max=limit).astype(held_as)


def setup_inputs(seed: int = 0, part: int = 0) -> dict:
    seeds = jax.random.split(jax.random.key(seed), 9)
    part_keys = jax.random.split(jax.random.fold_in(seeds[8], part), 9)
    return {
        "features": draw_features(jax.random.fold_in(jax.random.fold_in(seeds[8], part), 71), part),
        "init_noise": jnp.clip(jax.random.uniform(part_keys[1], (IMAGES, SIDE, SIDE, C), jnp.float32, -0.5, 0.5) * steps_of(part_keys[1], (IMAGES, SIDE, SIDE, C), ((0, 4),), -0.4, 0.0), -0.5, 0.5),
        "target": bell_draw(part_keys[2], (IMAGES, SIDE, SIDE, C), 1.0, 6.0, ((0, 4),)),
        "kernel": bell_draw(seeds[3], (BLOCKS, C, KK), KK ** -0.5, 0.875, ((0, 4),), jnp.float32),
        "norm_gain": jnp.clip(1.0 + 0.18 * jax.random.normal(seeds[4], (BLOCKS, C), jnp.float32), 0.1, 1.9),
        "layer_scale": jnp.clip(jnp.exp(math.log(1.0) - 1.609438 * jax.random.uniform(seeds[5], (BLOCKS, C), jnp.float32) ** steps_of(seeds[5], (BLOCKS, C), ((0, 4),), -0.2, 0.2)), 0.2, 1.0),
        "w_in": bell_draw(seeds[6], (BLOCKS, C, HID), C ** -0.5, 0.3125, ((0, 4), (1, 4))),
        "w_out": bell_draw(seeds[7], (BLOCKS, HID, C), HID ** -0.5, 0.15625, ((0, 4), (1, 4))),
    }


radius = 0.5
step_size = 0.625

def conv_norm(inputs, kernel, norm_gain):
    extent = inputs.shape[1]
    padded = jnp.pad(inputs, ((0, 0), (3, 3), (3, 3), (0, 0)))
    mixture = jnp.zeros_like(inputs)
    for tap_row in range(7):
        for tap_col in range(7):
            mixture = mixture + padded[:, tap_row:tap_row + extent, tap_col:tap_col + extent, :] * kernel[:, tap_row * 7 + tap_col]
    centre = mixture - lax.optimization_barrier(jnp.mean(mixture, axis=-1, keepdims=True))
    spread = lax.optimization_barrier(jnp.mean(centre * centre, axis=-1, keepdims=True))
    return centre * lax.rsqrt(spread + 1e-06) * norm_gain

def gelu_exact(values):
    return jax.nn.gelu(values, approximate=False)

def block_forward(inputs, kernel, norm_gain, layer_scale, w_in, w_out):
    widened = inputs.astype(jnp.float32)
    normed = conv_norm(widened, kernel, norm_gain).astype(jnp.bfloat16)
    channels = inputs.shape[-1]
    up_proj = jnp.dot(normed.reshape(-1, channels), w_in, preferred_element_type=jnp.float32)
    activated = gelu_exact(up_proj).astype(jnp.bfloat16)
    down_proj = jnp.dot(activated, w_out, preferred_element_type=jnp.float32).reshape(inputs.shape)
    result = (widened + layer_scale * down_proj).astype(jnp.bfloat16)
    return (result, normed, up_proj)

def block_backward(inputs, normed, up_proj, grad_out, kernel, norm_gain, layer_scale, w_in, w_out, with_weights):
    channels = inputs.shape[-1]
    outer_grad = grad_out.astype(jnp.float32)
    grad_down = (layer_scale * outer_grad).astype(jnp.bfloat16).reshape(-1, channels)
    grad_act = jnp.dot(grad_down, w_out.T, preferred_element_type=jnp.float32)
    unused_value, gelu_back = jax.vjp(gelu_exact, up_proj)
    grad_up = gelu_back(grad_act)[0].astype(jnp.bfloat16)
    grad_normed = jnp.dot(grad_up, w_in.T, preferred_element_type=jnp.float32).reshape(inputs.shape)
    unused_norm, norm_back = jax.vjp(conv_norm, inputs.astype(jnp.float32), kernel, norm_gain)
    grad_inputs, grad_kern, unused_gain = norm_back(grad_normed)
    grad_in = (outer_grad + grad_inputs).astype(jnp.bfloat16)
    if not with_weights:
        return (grad_in, ())
    activated = gelu_exact(up_proj).astype(jnp.bfloat16)
    grad_first = jnp.dot(normed.reshape(-1, channels).T, grad_up, preferred_element_type=jnp.float32)
    grad_second = jnp.dot(activated.T, grad_down, preferred_element_type=jnp.float32)
    return (grad_in, (grad_kern, grad_first, grad_second))

def network_forward(inputs, kernel, norm_gain, layer_scale, w_in, w_out):
    stored = []
    for block_idx in range(BLOCKS):
        stored.append(inputs)
        inputs, unused_normed, unused_up = block_forward(inputs, kernel[block_idx], norm_gain[block_idx], layer_scale[block_idx], w_in[block_idx], w_out[block_idx])
    return (inputs, stored)

def network_backward(stored, seed_grad, kernel, norm_gain, layer_scale, w_in, w_out, with_weights):
    grad_list = []
    for block_idx in reversed(range(BLOCKS)):
        unused_out, normed, up_proj = block_forward(stored[block_idx], kernel[block_idx], norm_gain[block_idx], layer_scale[block_idx], w_in[block_idx], w_out[block_idx])
        seed_grad, grads_now = block_backward(stored[block_idx], normed, up_proj, seed_grad, kernel[block_idx], norm_gain[block_idx], layer_scale[block_idx], w_in[block_idx], w_out[block_idx], with_weights)
        grad_list.insert(0, grads_now)
    return (seed_grad, grad_list)

def reference(features, init_noise, target, kernel, norm_gain, layer_scale, w_in, w_out):
    factor = 1.0 / math.sqrt(TOKENS)
    clean_in = (features.astype(jnp.float32) + init_noise).astype(jnp.bfloat16)
    outputs, stored = network_forward(clean_in, kernel, norm_gain, layer_scale, w_in, w_out)
    seed_grads = ((outputs.astype(jnp.float32) - target.astype(jnp.float32)) * factor).astype(jnp.bfloat16)
    slope_in, unused_list = network_backward(stored, seed_grads, kernel, norm_gain, layer_scale, w_in, w_out, False)
    slope = slope_in.astype(jnp.float32)
    rms_value = jnp.sqrt(lax.optimization_barrier(jnp.mean(slope * slope, axis=(1, 2, 3), keepdims=True)) + 1e-06)
    delta_step = jnp.clip(init_noise + step_size * jnp.tanh(slope / rms_value), -radius, radius)
    adverse = (features.astype(jnp.float32) + delta_step).astype(jnp.bfloat16)
    outputs_adv, stored_adv = network_forward(adverse, kernel, norm_gain, layer_scale, w_in, w_out)
    seed_adv = ((outputs_adv.astype(jnp.float32) - target.astype(jnp.float32)) * factor).astype(jnp.bfloat16)
    unused_grad, grad_list = network_backward(stored_adv, seed_adv, kernel, norm_gain, layer_scale, w_in, w_out, True)
    grad_kernel = jnp.stack([member[0] for member in grad_list])
    grad_w_in = jnp.stack([member[1] for member in grad_list])
    grad_w_out = jnp.stack([member[2] for member in grad_list])
    return (grad_kernel, grad_w_in, grad_w_out)
```

```python
import math

import jax
import jax.numpy as jnp
from jax import lax
from jax.sharding import PartitionSpec as P

MICRO = 4


radius = 0.5
step_size = 0.625


def from_behind(block, axis, distance):
    devices = range(lax.axis_size(axis))
    route = [(i - distance, i) for i in devices if i - distance in devices]
    return lax.ppermute(block, axis, route)


def conv_norm(inputs, kernel, norm_gain):
    extent = inputs.shape[1]
    padded = jnp.pad(inputs, ((0, 0), (3, 3), (3, 3), (0, 0)))
    mixture = jnp.zeros_like(inputs)
    for tap_row in range(7):
        for tap_col in range(7):
            mixture = (
                mixture
                + padded[:, tap_row : tap_row + extent, tap_col : tap_col + extent, :]
                * kernel[:, tap_row * 7 + tap_col]
            )
    centre = mixture - jnp.mean(mixture, axis=-1, keepdims=True)
    spread = jnp.mean(centre * centre, axis=-1, keepdims=True)
    return centre * lax.rsqrt(spread + 1e-06) * norm_gain


def gelu_exact(values):
    return jax.nn.gelu(values, approximate=False)


def block_forward(inputs, kernel, norm_gain, layer_scale, w_in, w_out):
    widened = inputs.astype(jnp.float32)
    normed = conv_norm(widened, kernel, norm_gain).astype(jnp.bfloat16)
    channels = inputs.shape[-1]
    up_proj = jnp.dot(normed.reshape(-1, channels), w_in, preferred_element_type=jnp.float32)
    activated = gelu_exact(up_proj).astype(jnp.bfloat16)
    down_proj = jnp.dot(activated, w_out, preferred_element_type=jnp.float32).reshape(inputs.shape)
    result = (widened + layer_scale * down_proj).astype(jnp.bfloat16)
    return (result, normed, up_proj)


def block_backward(
    inputs, normed, up_proj, grad_out, kernel, norm_gain, layer_scale, w_in, w_out, with_weights
):
    channels = inputs.shape[-1]
    outer_grad = grad_out.astype(jnp.float32)
    grad_down = (layer_scale * outer_grad).astype(jnp.bfloat16).reshape(-1, channels)
    grad_act = jnp.dot(grad_down, w_out.T, preferred_element_type=jnp.float32)
    unused_value, gelu_back = jax.vjp(gelu_exact, up_proj)
    grad_up = gelu_back(grad_act)[0].astype(jnp.bfloat16)
    grad_normed = jnp.dot(grad_up, w_in.T, preferred_element_type=jnp.float32).reshape(inputs.shape)
    unused_norm, norm_back = jax.vjp(conv_norm, inputs.astype(jnp.float32), kernel, norm_gain)
    grad_inputs, grad_kern, unused_gain = norm_back(grad_normed)
    grad_in = (outer_grad + grad_inputs).astype(jnp.bfloat16)
    if not with_weights:
        return (grad_in, ())
    activated = gelu_exact(up_proj).astype(jnp.bfloat16)
    grad_first = jnp.dot(
        normed.reshape(-1, channels).T, grad_up, preferred_element_type=jnp.float32
    )
    grad_second = jnp.dot(activated.T, grad_down, preferred_element_type=jnp.float32)
    return (grad_in, (grad_kern, grad_first, grad_second))


def section_forward(values, params):
    kernel, norm_gain, layer_scale, w_in, w_out = params
    inputs_list, normed_list, up_list = ([], [], [])
    inputs_list.append(values)
    values, normed, up_proj = block_forward(
        values, kernel[0], norm_gain[0], layer_scale[0], w_in[0], w_out[0]
    )
    normed_list.append(normed)
    up_list.append(up_proj)
    return (values, (jnp.stack(inputs_list), jnp.stack(normed_list), jnp.stack(up_list)))


def section_backward(entry_now, grad_now, params, with_weights):
    kernel, norm_gain, layer_scale, w_in, w_out = params
    inputs_all, normed_all, up_all = entry_now
    results = []
    for layer_idx in reversed(range(kernel.shape[0])):
        grad_now, grads_now = block_backward(
            inputs_all[layer_idx],
            normed_all[layer_idx],
            up_all[layer_idx],
            grad_now,
            kernel[layer_idx],
            norm_gain[layer_idx],
            layer_scale[layer_idx],
            w_in[layer_idx],
            w_out[layer_idx],
            with_weights,
        )
        results.insert(0, grads_now)
    if not with_weights:
        return (grad_now, ())
    return (
        grad_now,
        tuple((jnp.stack([member[part_idx] for member in results]) for part_idx in range(3))),
    )


def run_forward(inputs, params, pieces):
    sections = lax.axis_size("section")
    section_idx = lax.axis_index("section")
    kernel, norm_gain, layer_scale, w_in, w_out = params
    depth = kernel.shape[0]
    per_piece = inputs.shape[0] // pieces
    pieces_in = inputs.reshape((pieces, per_piece) + inputs.shape[1:])
    rows_piece = per_piece * inputs.shape[1] * inputs.shape[2]
    saved = (
        jnp.zeros((pieces, depth) + pieces_in.shape[1:], jnp.bfloat16),
        jnp.zeros((pieces, depth) + pieces_in.shape[1:], jnp.bfloat16),
        jnp.zeros((pieces, depth, rows_piece, w_in.shape[-1]), jnp.float32),
    )
    outputs = jnp.zeros_like(pieces_in)

    def advance(values):
        return section_forward(values, params)

    def pass_by(values):
        return (values, tuple((jnp.zeros(member.shape[1:], member.dtype) for member in saved)))

    def tick_fn(tick_idx, carry_in):
        buffer, saved_now, outputs_now = carry_in
        slot_raw = tick_idx - section_idx
        active = (slot_raw >= 0) & (slot_raw < pieces)
        slot_idx = jnp.clip(slot_raw, 0, pieces - 1)
        fed_in = jnp.where(
            section_idx == 0,
            lax.dynamic_index_in_dim(pieces_in, slot_idx, 0, keepdims=False),
            buffer,
        )
        result, entry_now = lax.cond(active, advance, pass_by, fed_in)
        saved_now = tuple(
            (
                jnp.where(
                    active, lax.dynamic_update_index_in_dim(previous, fresh, slot_idx, 0), previous
                )
                for previous, fresh in zip(saved_now, entry_now)
            )
        )
        at_end = active & (section_idx == sections - 1)
        outputs_now = jnp.where(
            at_end, lax.dynamic_update_index_in_dim(outputs_now, result, slot_idx, 0), outputs_now
        )
        buffer = from_behind(result, "section", 1)
        return (buffer, saved_now, outputs_now)

    start_carry = (jnp.zeros_like(pieces_in[0]), saved, outputs)
    unused_buffer, saved, outputs = lax.fori_loop(0, pieces + sections - 1, tick_fn, start_carry)
    return (outputs.reshape(inputs.shape), saved)


def run_backward(saved, seed_grads, params, pieces, with_weights):
    sections = lax.axis_size("section")
    section_idx = lax.axis_index("section")
    kernel, norm_gain, layer_scale, w_in, w_out = params
    per_piece = seed_grads.shape[0] // pieces
    pieces_in = seed_grads.reshape((pieces, per_piece) + seed_grads.shape[1:])
    returned = jnp.zeros_like(pieces_in)
    if with_weights:
        totals = (
            jnp.zeros(kernel.shape, jnp.float32),
            jnp.zeros(w_in.shape, jnp.float32),
            jnp.zeros(w_out.shape, jnp.float32),
        )
    else:
        totals = ()

    def advance(operands):
        return section_backward(operands[0], operands[1], params, with_weights)

    def pass_by(operands):
        return (operands[1], tuple((jnp.zeros_like(member) for member in totals)))

    def tick_fn(tick_idx, carry_in):
        buffer, returned_now, totals_now = carry_in
        slot_raw = tick_idx - (sections - 1 - section_idx)
        active = (slot_raw >= 0) & (slot_raw < pieces)
        slot_idx = jnp.clip(slot_raw, 0, pieces - 1)
        entry_now = tuple(
            (lax.dynamic_index_in_dim(member, slot_idx, 0, keepdims=False) for member in saved)
        )
        fed_in = jnp.where(
            section_idx == sections - 1,
            lax.dynamic_index_in_dim(pieces_in, slot_idx, 0, keepdims=False),
            buffer,
        )
        grad_in, grads_now = lax.cond(active, advance, pass_by, (entry_now, fed_in))
        totals_now = tuple((previous + fresh for previous, fresh in zip(totals_now, grads_now)))
        at_first = active & (section_idx == 0)
        returned_now = jnp.where(
            at_first,
            lax.dynamic_update_index_in_dim(returned_now, grad_in, slot_idx, 0),
            returned_now,
        )
        buffer = from_behind(grad_in, "section", -1)
        return (buffer, returned_now, totals_now)

    start_carry = (jnp.zeros_like(pieces_in[0]), returned, totals)
    unused_buffer, returned, totals = lax.fori_loop(0, pieces + sections - 1, tick_fn, start_carry)
    return (returned.reshape(seed_grads.shape), totals)


def gather_blocks(block, rows_axis):
    sections = lax.axis_size("section")
    whole = lax.all_gather(block, ("section", "dp"), axis=0, tiled=True)
    return whole.reshape((sections, -1) + whole.shape[2:])


def scatter_blocks(total):
    sections = lax.axis_size("section")
    groups = lax.axis_size("dp")
    split = total.reshape((sections * groups, total.shape[1] // groups) + total.shape[2:])
    return lax.psum_scatter(
        split.astype(jnp.bfloat16), ("section", "dp"), scatter_dimension=0, tiled=True
    ).astype(jnp.float32)


def network_forward(values, params):
    kernel, norm_gain, layer_scale, w_in, w_out = params
    stored = []
    for block_idx in range(kernel.shape[0]):
        inputs = values
        values, normed, up_proj = block_forward(
            inputs, kernel[block_idx], norm_gain[block_idx], layer_scale[block_idx],
            w_in[block_idx], w_out[block_idx],
        )
        stored.append((inputs, normed, up_proj))
    return values, stored


def network_backward(stored, grad_now, params, with_weights):
    kernel, norm_gain, layer_scale, w_in, w_out = params
    results = [None] * kernel.shape[0]
    for block_idx in reversed(range(kernel.shape[0])):
        inputs, normed, up_proj = stored[block_idx]
        grad_now, grads_now = block_backward(
            inputs, normed, up_proj, grad_now, kernel[block_idx], norm_gain[block_idx],
            layer_scale[block_idx], w_in[block_idx], w_out[block_idx], with_weights,
        )
        results[block_idx] = grads_now
    return grad_now, results


def per_device_flat(features, init_noise, target, kernel, norm_gain, layer_scale, w_in, w_out):
    sections = lax.axis_size("section")
    section_idx = lax.axis_index("section")
    groups = lax.axis_size("dp")
    factor = 1.0 / math.sqrt(features.shape[0] * features.shape[1] * features.shape[2] * groups)
    own = features.shape[0] // sections

    def mine(whole):
        return lax.dynamic_slice_in_dim(whole, section_idx * own, own, 0)

    features, init_noise, target = mine(features), mine(init_noise), mine(target)
    params = (
        lax.all_gather(kernel, "section", axis=0, tiled=True),
        lax.all_gather(norm_gain, "section", axis=0, tiled=True),
        lax.all_gather(layer_scale, "section", axis=0, tiled=True),
        gather_blocks(w_in, 1),
        gather_blocks(w_out, 1),
    )
    clean_in = (features.astype(jnp.float32) + init_noise).astype(jnp.bfloat16)
    outputs, stored = network_forward(clean_in, params)
    seed_grads = ((outputs.astype(jnp.float32) - target.astype(jnp.float32)) * factor).astype(
        jnp.bfloat16
    )
    slope_in, unused_list = network_backward(stored, seed_grads, params, False)
    slope = slope_in.astype(jnp.float32)
    rms_value = jnp.sqrt(jnp.mean(slope * slope, axis=(1, 2, 3), keepdims=True) + 1e-06)
    delta_step = jnp.clip(init_noise + step_size * jnp.tanh(slope / rms_value), -radius, radius)
    adverse = (features.astype(jnp.float32) + delta_step).astype(jnp.bfloat16)
    outputs_adv, stored_adv = network_forward(adverse, params)
    seed_adv = ((outputs_adv.astype(jnp.float32) - target.astype(jnp.float32)) * factor).astype(
        jnp.bfloat16
    )
    unused_grad, grad_list = network_backward(stored_adv, seed_adv, params, True)
    return tuple(
        scatter_blocks(jnp.stack([grads[part_idx] for grads in grad_list]))
        for part_idx in range(3)
    )


def per_device(features, init_noise, target, kernel, norm_gain, layer_scale, w_in, w_out):
    full_in, full_out = (
        lax.all_gather(w_in, "dp", axis=1, tiled=True),
        lax.all_gather(w_out, "dp", axis=1, tiled=True),
    )
    params = (kernel, norm_gain, layer_scale, full_in, full_out)
    pieces = MICRO // 2
    groups = lax.axis_size("dp")
    factor = 1.0 / math.sqrt(features.shape[0] * features.shape[1] * features.shape[2] * groups)
    clean_in = (features.astype(jnp.float32) + init_noise).astype(jnp.bfloat16)
    outputs, saved = run_forward(clean_in, params, pieces)
    seed_grads = ((outputs.astype(jnp.float32) - target.astype(jnp.float32)) * factor).astype(
        jnp.bfloat16
    )
    slope_in, unused_totals = run_backward(saved, seed_grads, params, pieces, False)
    slope = slope_in.astype(jnp.float32)
    rms_value = jnp.sqrt(jnp.mean(slope * slope, axis=(1, 2, 3), keepdims=True) + 1e-06)
    delta_step = jnp.clip(init_noise + step_size * jnp.tanh(slope / rms_value), -radius, radius)
    adverse = (features.astype(jnp.float32) + delta_step).astype(jnp.bfloat16)
    outputs_adv, saved_adv = run_forward(adverse, params, pieces)
    seed_adv = ((outputs_adv.astype(jnp.float32) - target.astype(jnp.float32)) * factor).astype(
        jnp.bfloat16
    )
    unused_grad, totals = run_backward(saved_adv, seed_adv, params, pieces, True)
    grad_kern, grad_first, grad_second = totals
    summed = (
        lax.psum_scatter(
            grad_kern.astype(jnp.bfloat16), "dp", scatter_dimension=1, tiled=True
        ).astype(jnp.float32),
        lax.psum_scatter(
            grad_first.astype(jnp.bfloat16), "dp", scatter_dimension=1, tiled=True
        ).astype(jnp.float32),
        lax.psum_scatter(
            grad_second.astype(jnp.bfloat16), "dp", scatter_dimension=1, tiled=True
        ).astype(jnp.float32),
    )
    return (summed[0], summed[1], summed[2])


def solution(mesh):
    def chosen(features, *rest):
        if features.shape[0] % mesh.shape["section"] == 0:
            return per_device_flat(features, *rest)
        return per_device(features, *rest)

    placed = (
        P(("group", "dp"), None, None, None),
        P(("group", "dp"), None, None, None),
        P(("group", "dp"), None, None, None),
        P("section", None, None),
        P("section", None),
        P("section", None),
        P("section", "dp", None),
        P("section", "dp", None),
    )
    return jax.shard_map(
        chosen,
        mesh=mesh,
        in_specs=placed,
        out_specs=(
            P(("group", "section"), "dp", None),
            P(("group", "section"), "dp", None),
            P(("group", "section"), "dp", None),
        ),
        check_vma=False,
    )
```

```python
import math

import jax
import jax.numpy as jnp
from jax import lax
from jax.sharding import PartitionSpec as P

MICRO = 4


radius = 0.5
step_size = 0.625


def from_behind(block, axis, distance):
    devices = range(lax.axis_size(axis))
    route = [(i - distance, i) for i in devices if i - distance in devices]
    return lax.ppermute(block, axis, route)


def conv_norm(inputs, kernel, norm_gain):
    extent = inputs.shape[1]
    padded = jnp.pad(inputs, ((0, 0), (3, 3), (3, 3), (0, 0)))
    mixture = jnp.zeros_like(inputs)
    for tap_row in range(7):
        for tap_col in range(7):
            mixture = (
                mixture
                + padded[:, tap_row : tap_row + extent, tap_col : tap_col + extent, :]
                * kernel[:, tap_row * 7 + tap_col]
            )
    centre = mixture - jnp.mean(mixture, axis=-1, keepdims=True)
    spread = jnp.mean(centre * centre, axis=-1, keepdims=True)
    return centre * lax.rsqrt(spread + 1e-06) * norm_gain


def gelu_exact(values):
    return jax.nn.gelu(values, approximate=False)


def block_forward(inputs, kernel, norm_gain, layer_scale, w_in, w_out):
    widened = inputs.astype(jnp.float32)
    normed = conv_norm(widened, kernel, norm_gain).astype(jnp.bfloat16)
    channels = inputs.shape[-1]
    up_proj = jnp.dot(normed.reshape(-1, channels), w_in, preferred_element_type=jnp.float32)
    activated = gelu_exact(up_proj).astype(jnp.bfloat16)
    down_proj = jnp.dot(activated, w_out, preferred_element_type=jnp.float32).reshape(inputs.shape)
    result = (widened + layer_scale * down_proj).astype(jnp.bfloat16)
    return (result, normed, up_proj)


def block_backward(
    inputs, normed, up_proj, grad_out, kernel, norm_gain, layer_scale, w_in, w_out, with_weights
):
    channels = inputs.shape[-1]
    outer_grad = grad_out.astype(jnp.float32)
    grad_down = (layer_scale * outer_grad).astype(jnp.bfloat16).reshape(-1, channels)
    grad_act = jnp.dot(grad_down, w_out.T, preferred_element_type=jnp.float32)
    unused_value, gelu_back = jax.vjp(gelu_exact, up_proj)
    grad_up = gelu_back(grad_act)[0].astype(jnp.bfloat16)
    grad_normed = jnp.dot(grad_up, w_in.T, preferred_element_type=jnp.float32).reshape(inputs.shape)
    unused_norm, norm_back = jax.vjp(conv_norm, inputs.astype(jnp.float32), kernel, norm_gain)
    grad_inputs, grad_kern, unused_gain = norm_back(grad_normed)
    grad_in = (outer_grad + grad_inputs).astype(jnp.bfloat16)
    if not with_weights:
        return (grad_in, ())
    activated = gelu_exact(up_proj).astype(jnp.bfloat16)
    grad_first = jnp.dot(
        normed.reshape(-1, channels).T, grad_up, preferred_element_type=jnp.float32
    )
    grad_second = jnp.dot(activated.T, grad_down, preferred_element_type=jnp.float32)
    return (grad_in, (grad_kern, grad_first, grad_second))


def section_forward(values, params):
    kernel, norm_gain, layer_scale, w_in, w_out = params
    inputs_list, normed_list, up_list = ([], [], [])
    inputs_list.append(values)
    values, normed, up_proj = block_forward(
        values, kernel[0], norm_gain[0], layer_scale[0], w_in[0], w_out[0]
    )
    normed_list.append(normed)
    up_list.append(up_proj)
    return (values, (jnp.stack(inputs_list), jnp.stack(normed_list), jnp.stack(up_list)))


def section_backward(entry_now, grad_now, params, with_weights):
    kernel, norm_gain, layer_scale, w_in, w_out = params
    inputs_all, normed_all, up_all = entry_now
    results = []
    for layer_idx in reversed(range(kernel.shape[0])):
        grad_now, grads_now = block_backward(
            inputs_all[layer_idx],
            normed_all[layer_idx],
            up_all[layer_idx],
            grad_now,
            kernel[layer_idx],
            norm_gain[layer_idx],
            layer_scale[layer_idx],
            w_in[layer_idx],
            w_out[layer_idx],
            with_weights,
        )
        results.insert(0, grads_now)
    if not with_weights:
        return (grad_now, ())
    return (
        grad_now,
        tuple((jnp.stack([member[part_idx] for member in results]) for part_idx in range(3))),
    )


def run_forward(inputs, params, pieces):
    sections = lax.axis_size("section")
    section_idx = lax.axis_index("section")
    kernel, norm_gain, layer_scale, w_in, w_out = params
    depth = kernel.shape[0]
    per_piece = inputs.shape[0] // pieces
    pieces_in = inputs.reshape((pieces, per_piece) + inputs.shape[1:])
    rows_piece = per_piece * inputs.shape[1] * inputs.shape[2]
    saved = (
        jnp.zeros((pieces, depth) + pieces_in.shape[1:], jnp.bfloat16),
        jnp.zeros((pieces, depth) + pieces_in.shape[1:], jnp.bfloat16),
        jnp.zeros((pieces, depth, rows_piece, w_in.shape[-1]), jnp.float32),
    )
    outputs = jnp.zeros_like(pieces_in)

    def advance(values):
        return section_forward(values, params)

    def pass_by(values):
        return (values, tuple((jnp.zeros(member.shape[1:], member.dtype) for member in saved)))

    def tick_fn(tick_idx, carry_in):
        buffer, saved_now, outputs_now = carry_in
        slot_raw = tick_idx - section_idx
        active = (slot_raw >= 0) & (slot_raw < pieces)
        slot_idx = jnp.clip(slot_raw, 0, pieces - 1)
        fed_in = jnp.where(
            section_idx == 0,
            lax.dynamic_index_in_dim(pieces_in, slot_idx, 0, keepdims=False),
            buffer,
        )
        result, entry_now = lax.cond(active, advance, pass_by, fed_in)
        saved_now = tuple(
            (
                jnp.where(
                    active, lax.dynamic_update_index_in_dim(previous, fresh, slot_idx, 0), previous
                )
                for previous, fresh in zip(saved_now, entry_now)
            )
        )
        at_end = active & (section_idx == sections - 1)
        outputs_now = jnp.where(
            at_end, lax.dynamic_update_index_in_dim(outputs_now, result, slot_idx, 0), outputs_now
        )
        buffer = from_behind(result, "section", 1)
        return (buffer, saved_now, outputs_now)

    start_carry = (jnp.zeros_like(pieces_in[0]), saved, outputs)
    unused_buffer, saved, outputs = lax.fori_loop(0, pieces + sections - 1, tick_fn, start_carry)
    return (outputs.reshape(inputs.shape), saved)


def run_backward(saved, seed_grads, params, pieces, with_weights):
    sections = lax.axis_size("section")
    section_idx = lax.axis_index("section")
    kernel, norm_gain, layer_scale, w_in, w_out = params
    per_piece = seed_grads.shape[0] // pieces
    pieces_in = seed_grads.reshape((pieces, per_piece) + seed_grads.shape[1:])
    returned = jnp.zeros_like(pieces_in)
    if with_weights:
        totals = (
            jnp.zeros(kernel.shape, jnp.float32),
            jnp.zeros(w_in.shape, jnp.float32),
            jnp.zeros(w_out.shape, jnp.float32),
        )
    else:
        totals = ()

    def advance(operands):
        return section_backward(operands[0], operands[1], params, with_weights)

    def pass_by(operands):
        return (operands[1], tuple((jnp.zeros_like(member) for member in totals)))

    def tick_fn(tick_idx, carry_in):
        buffer, returned_now, totals_now = carry_in
        slot_raw = tick_idx - (sections - 1 - section_idx)
        active = (slot_raw >= 0) & (slot_raw < pieces)
        slot_idx = jnp.clip(slot_raw, 0, pieces - 1)
        entry_now = tuple(
            (lax.dynamic_index_in_dim(member, slot_idx, 0, keepdims=False) for member in saved)
        )
        fed_in = jnp.where(
            section_idx == sections - 1,
            lax.dynamic_index_in_dim(pieces_in, slot_idx, 0, keepdims=False),
            buffer,
        )
        grad_in, grads_now = lax.cond(active, advance, pass_by, (entry_now, fed_in))
        totals_now = tuple((previous + fresh for previous, fresh in zip(totals_now, grads_now)))
        at_first = active & (section_idx == 0)
        returned_now = jnp.where(
            at_first,
            lax.dynamic_update_index_in_dim(returned_now, grad_in, slot_idx, 0),
            returned_now,
        )
        buffer = from_behind(grad_in, "section", -1)
        return (buffer, returned_now, totals_now)

    start_carry = (jnp.zeros_like(pieces_in[0]), returned, totals)
    unused_buffer, returned, totals = lax.fori_loop(0, pieces + sections - 1, tick_fn, start_carry)
    return (returned.reshape(seed_grads.shape), totals)


def gather_blocks(block, rows_axis):
    sections = lax.axis_size("section")
    whole = lax.all_gather(block, ("section", "dp"), axis=0, tiled=True)
    return whole.reshape((sections, -1) + whole.shape[2:])


def split_exact(values):
    high = values.astype(jnp.bfloat16)
    rest = values - high.astype(jnp.float32)
    middle = rest.astype(jnp.bfloat16)
    low = (rest - middle.astype(jnp.float32)).astype(jnp.bfloat16)
    return jnp.concatenate([high, middle, low], axis=-1)


def join_exact(packed, width):
    terms = [packed[..., i * width : (i + 1) * width].astype(jnp.float32) for i in range(3)]
    return (terms[0] + terms[1]) + terms[2]


def gather_params(kernel, norm_gain, layer_scale, w_in, w_out):
    groups = lax.axis_size("dp")
    dp_idx = lax.axis_index("dp")
    rows = w_in.shape[1]
    small = jnp.concatenate([kernel[0], norm_gain[0][:, None], layer_scale[0][:, None]], axis=-1)
    small = lax.dynamic_slice_in_dim(small, dp_idx * rows, rows, 0)
    width = small.shape[-1]
    packed = split_exact(small)
    pad = (-(w_in.shape[-1] + packed.shape[-1])) % 128
    packed = jnp.pad(packed, ((0, 0), (0, pad)))
    joined = jnp.concatenate([w_in[0], packed], axis=-1)[None]
    whole = gather_blocks(joined, 1)
    full_in = whole[..., : w_in.shape[-1]]
    small_all = join_exact(whole[..., w_in.shape[-1] :], width)
    taps = kernel.shape[-1]
    return (
        small_all[..., :taps],
        small_all[..., taps],
        small_all[..., taps + 1],
        full_in,
        gather_blocks(w_out, 1),
    )


def scatter_blocks(total):
    sections = lax.axis_size("section")
    groups = lax.axis_size("dp")
    split = total.reshape((sections * groups, total.shape[1] // groups) + total.shape[2:])
    return lax.psum_scatter(
        split.astype(jnp.bfloat16), ("section", "dp"), scatter_dimension=0, tiled=True
    ).astype(jnp.float32)


def network_forward(values, params):
    kernel, norm_gain, layer_scale, w_in, w_out = params
    stored = []
    for block_idx in range(kernel.shape[0]):
        inputs = values
        values, normed, up_proj = block_forward(
            inputs, kernel[block_idx], norm_gain[block_idx], layer_scale[block_idx],
            w_in[block_idx], w_out[block_idx],
        )
        stored.append((inputs, normed, up_proj))
    return values, stored


def network_backward(stored, grad_now, params, with_weights):
    kernel, norm_gain, layer_scale, w_in, w_out = params
    results = [None] * kernel.shape[0]
    for block_idx in reversed(range(kernel.shape[0])):
        inputs, normed, up_proj = stored[block_idx]
        grad_now, grads_now = block_backward(
            inputs, normed, up_proj, grad_now, kernel[block_idx], norm_gain[block_idx],
            layer_scale[block_idx], w_in[block_idx], w_out[block_idx], with_weights,
        )
        results[block_idx] = grads_now
    return grad_now, results


def per_device_flat(features, init_noise, target, kernel, norm_gain, layer_scale, w_in, w_out):
    sections = lax.axis_size("section")
    section_idx = lax.axis_index("section")
    groups = lax.axis_size("dp")
    factor = 1.0 / math.sqrt(features.shape[0] * features.shape[1] * features.shape[2] * groups)
    own = features.shape[0] // sections

    def mine(whole):
        return lax.dynamic_slice_in_dim(whole, section_idx * own, own, 0)

    features, init_noise, target = mine(features), mine(init_noise), mine(target)
    params = gather_params(kernel, norm_gain, layer_scale, w_in, w_out)
    clean_in = (features.astype(jnp.float32) + init_noise).astype(jnp.bfloat16)
    outputs, stored = network_forward(clean_in, params)
    seed_grads = ((outputs.astype(jnp.float32) - target.astype(jnp.float32)) * factor).astype(
        jnp.bfloat16
    )
    slope_in, unused_list = network_backward(stored, seed_grads, params, False)
    slope = slope_in.astype(jnp.float32)
    rms_value = jnp.sqrt(jnp.mean(slope * slope, axis=(1, 2, 3), keepdims=True) + 1e-06)
    delta_step = jnp.clip(init_noise + step_size * jnp.tanh(slope / rms_value), -radius, radius)
    adverse = (features.astype(jnp.float32) + delta_step).astype(jnp.bfloat16)
    outputs_adv, stored_adv = network_forward(adverse, params)
    seed_adv = ((outputs_adv.astype(jnp.float32) - target.astype(jnp.float32)) * factor).astype(
        jnp.bfloat16
    )
    unused_grad, grad_list = network_backward(stored_adv, seed_adv, params, True)
    return tuple(
        scatter_blocks(jnp.stack([grads[part_idx] for grads in grad_list]))
        for part_idx in range(3)
    )


def per_device(features, init_noise, target, kernel, norm_gain, layer_scale, w_in, w_out):
    full_in, full_out = (
        lax.all_gather(w_in, "dp", axis=1, tiled=True),
        lax.all_gather(w_out, "dp", axis=1, tiled=True),
    )
    params = (kernel, norm_gain, layer_scale, full_in, full_out)
    pieces = MICRO // 2
    groups = lax.axis_size("dp")
    factor = 1.0 / math.sqrt(features.shape[0] * features.shape[1] * features.shape[2] * groups)
    clean_in = (features.astype(jnp.float32) + init_noise).astype(jnp.bfloat16)
    outputs, saved = run_forward(clean_in, params, pieces)
    seed_grads = ((outputs.astype(jnp.float32) - target.astype(jnp.float32)) * factor).astype(
        jnp.bfloat16
    )
    slope_in, unused_totals = run_backward(saved, seed_grads, params, pieces, False)
    slope = slope_in.astype(jnp.float32)
    rms_value = jnp.sqrt(jnp.mean(slope * slope, axis=(1, 2, 3), keepdims=True) + 1e-06)
    delta_step = jnp.clip(init_noise + step_size * jnp.tanh(slope / rms_value), -radius, radius)
    adverse = (features.astype(jnp.float32) + delta_step).astype(jnp.bfloat16)
    outputs_adv, saved_adv = run_forward(adverse, params, pieces)
    seed_adv = ((outputs_adv.astype(jnp.float32) - target.astype(jnp.float32)) * factor).astype(
        jnp.bfloat16
    )
    unused_grad, totals = run_backward(saved_adv, seed_adv, params, pieces, True)
    grad_kern, grad_first, grad_second = totals
    summed = (
        lax.psum_scatter(
            grad_kern.astype(jnp.bfloat16), "dp", scatter_dimension=1, tiled=True
        ).astype(jnp.float32),
        lax.psum_scatter(
            grad_first.astype(jnp.bfloat16), "dp", scatter_dimension=1, tiled=True
        ).astype(jnp.float32),
        lax.psum_scatter(
            grad_second.astype(jnp.bfloat16), "dp", scatter_dimension=1, tiled=True
        ).astype(jnp.float32),
    )
    return (summed[0], summed[1], summed[2])


def solution(mesh):
    def chosen(features, *rest):
        if features.shape[0] % mesh.shape["section"] == 0:
            return per_device_flat(features, *rest)
        return per_device(features, *rest)

    placed = (
        P(("group", "dp"), None, None, None),
        P(("group", "dp"), None, None, None),
        P(("group", "dp"), None, None, None),
        P("section", None, None),
        P("section", None),
        P("section", None),
        P("section", "dp", None),
        P("section", "dp", None),
    )
    return jax.shard_map(
        chosen,
        mesh=mesh,
        in_specs=placed,
        out_specs=(
            P(("group", "section"), "dp", None),
            P(("group", "section"), "dp", None),
            P(("group", "section"), "dp", None),
        ),
        check_vma=False,
    )
```

```python
import math

import jax
import jax.numpy as jnp
from jax import lax
from jax.sharding import PartitionSpec as P

MICRO = 4


radius = 0.5
step_size = 0.625


def from_behind(block, axis, distance):
    devices = range(lax.axis_size(axis))
    route = [(i - distance, i) for i in devices if i - distance in devices]
    return lax.ppermute(block, axis, route)


def conv_norm(inputs, kernel, norm_gain):
    extent = inputs.shape[1]
    padded = jnp.pad(inputs, ((0, 0), (3, 3), (3, 3), (0, 0)))
    mixture = jnp.zeros_like(inputs)
    for tap_row in range(7):
        for tap_col in range(7):
            mixture = (
                mixture
                + padded[:, tap_row : tap_row + extent, tap_col : tap_col + extent, :]
                * kernel[:, tap_row * 7 + tap_col]
            )
    centre = mixture - jnp.mean(mixture, axis=-1, keepdims=True)
    spread = jnp.mean(centre * centre, axis=-1, keepdims=True)
    return centre * lax.rsqrt(spread + 1e-06) * norm_gain


def gelu_exact(values):
    return jax.nn.gelu(values, approximate=False)


def block_forward(inputs, kernel, norm_gain, layer_scale, w_in, w_out):
    widened = inputs.astype(jnp.float32)
    normed = conv_norm(widened, kernel, norm_gain).astype(jnp.bfloat16)
    channels = inputs.shape[-1]
    up_proj = jnp.dot(normed.reshape(-1, channels), w_in, preferred_element_type=jnp.float32)
    activated = gelu_exact(up_proj).astype(jnp.bfloat16)
    down_proj = jnp.dot(activated, w_out, preferred_element_type=jnp.float32).reshape(inputs.shape)
    result = (widened + layer_scale * down_proj).astype(jnp.bfloat16)
    return (result, normed, up_proj)


def block_backward(
    inputs, normed, up_proj, grad_out, kernel, norm_gain, layer_scale, w_in, w_out, with_weights
):
    channels = inputs.shape[-1]
    outer_grad = grad_out.astype(jnp.float32)
    grad_down = (layer_scale * outer_grad).astype(jnp.bfloat16).reshape(-1, channels)
    grad_act = jnp.dot(grad_down, w_out.T, preferred_element_type=jnp.float32)
    unused_value, gelu_back = jax.vjp(gelu_exact, up_proj)
    grad_up = gelu_back(grad_act)[0].astype(jnp.bfloat16)
    grad_normed = jnp.dot(grad_up, w_in.T, preferred_element_type=jnp.float32).reshape(inputs.shape)
    unused_norm, norm_back = jax.vjp(conv_norm, inputs.astype(jnp.float32), kernel, norm_gain)
    grad_inputs, grad_kern, unused_gain = norm_back(grad_normed)
    grad_in = (outer_grad + grad_inputs).astype(jnp.bfloat16)
    if not with_weights:
        return (grad_in, ())
    activated = gelu_exact(up_proj).astype(jnp.bfloat16)
    grad_first = jnp.dot(
        normed.reshape(-1, channels).T, grad_up, preferred_element_type=jnp.float32
    )
    grad_second = jnp.dot(activated.T, grad_down, preferred_element_type=jnp.float32)
    return (grad_in, (grad_kern, grad_first, grad_second))


def section_forward(values, params):
    kernel, norm_gain, layer_scale, w_in, w_out = params
    inputs_list, normed_list, up_list = ([], [], [])
    inputs_list.append(values)
    values, normed, up_proj = block_forward(
        values, kernel[0], norm_gain[0], layer_scale[0], w_in[0], w_out[0]
    )
    normed_list.append(normed)
    up_list.append(up_proj)
    return (values, (jnp.stack(inputs_list), jnp.stack(normed_list), jnp.stack(up_list)))


def section_backward(entry_now, grad_now, params, with_weights):
    kernel, norm_gain, layer_scale, w_in, w_out = params
    inputs_all, normed_all, up_all = entry_now
    results = []
    for layer_idx in reversed(range(kernel.shape[0])):
        grad_now, grads_now = block_backward(
            inputs_all[layer_idx],
            normed_all[layer_idx],
            up_all[layer_idx],
            grad_now,
            kernel[layer_idx],
            norm_gain[layer_idx],
            layer_scale[layer_idx],
            w_in[layer_idx],
            w_out[layer_idx],
            with_weights,
        )
        results.insert(0, grads_now)
    if not with_weights:
        return (grad_now, ())
    return (
        grad_now,
        tuple((jnp.stack([member[part_idx] for member in results]) for part_idx in range(3))),
    )


def run_forward(inputs, params, pieces):
    sections = lax.axis_size("section")
    section_idx = lax.axis_index("section")
    kernel, norm_gain, layer_scale, w_in, w_out = params
    depth = kernel.shape[0]
    per_piece = inputs.shape[0] // pieces
    pieces_in = inputs.reshape((pieces, per_piece) + inputs.shape[1:])
    rows_piece = per_piece * inputs.shape[1] * inputs.shape[2]
    saved = (
        jnp.zeros((pieces, depth) + pieces_in.shape[1:], jnp.bfloat16),
        jnp.zeros((pieces, depth) + pieces_in.shape[1:], jnp.bfloat16),
        jnp.zeros((pieces, depth, rows_piece, w_in.shape[-1]), jnp.float32),
    )
    outputs = jnp.zeros_like(pieces_in)

    def advance(values):
        return section_forward(values, params)

    def pass_by(values):
        return (values, tuple((jnp.zeros(member.shape[1:], member.dtype) for member in saved)))

    def tick_fn(tick_idx, carry_in):
        buffer, saved_now, outputs_now = carry_in
        slot_raw = tick_idx - section_idx
        active = (slot_raw >= 0) & (slot_raw < pieces)
        slot_idx = jnp.clip(slot_raw, 0, pieces - 1)
        fed_in = jnp.where(
            section_idx == 0,
            lax.dynamic_index_in_dim(pieces_in, slot_idx, 0, keepdims=False),
            buffer,
        )
        result, entry_now = lax.cond(active, advance, pass_by, fed_in)
        saved_now = tuple(
            (
                jnp.where(
                    active, lax.dynamic_update_index_in_dim(previous, fresh, slot_idx, 0), previous
                )
                for previous, fresh in zip(saved_now, entry_now)
            )
        )
        at_end = active & (section_idx == sections - 1)
        outputs_now = jnp.where(
            at_end, lax.dynamic_update_index_in_dim(outputs_now, result, slot_idx, 0), outputs_now
        )
        buffer = from_behind(result, "section", 1)
        return (buffer, saved_now, outputs_now)

    start_carry = (jnp.zeros_like(pieces_in[0]), saved, outputs)
    unused_buffer, saved, outputs = lax.fori_loop(0, pieces + sections - 1, tick_fn, start_carry)
    return (outputs.reshape(inputs.shape), saved)


def run_backward(saved, seed_grads, params, pieces, with_weights):
    sections = lax.axis_size("section")
    section_idx = lax.axis_index("section")
    kernel, norm_gain, layer_scale, w_in, w_out = params
    per_piece = seed_grads.shape[0] // pieces
    pieces_in = seed_grads.reshape((pieces, per_piece) + seed_grads.shape[1:])
    returned = jnp.zeros_like(pieces_in)
    if with_weights:
        totals = (
            jnp.zeros(kernel.shape, jnp.float32),
            jnp.zeros(w_in.shape, jnp.float32),
            jnp.zeros(w_out.shape, jnp.float32),
        )
    else:
        totals = ()

    def advance(operands):
        return section_backward(operands[0], operands[1], params, with_weights)

    def pass_by(operands):
        return (operands[1], tuple((jnp.zeros_like(member) for member in totals)))

    def tick_fn(tick_idx, carry_in):
        buffer, returned_now, totals_now = carry_in
        slot_raw = tick_idx - (sections - 1 - section_idx)
        active = (slot_raw >= 0) & (slot_raw < pieces)
        slot_idx = jnp.clip(slot_raw, 0, pieces - 1)
        entry_now = tuple(
            (lax.dynamic_index_in_dim(member, slot_idx, 0, keepdims=False) for member in saved)
        )
        fed_in = jnp.where(
            section_idx == sections - 1,
            lax.dynamic_index_in_dim(pieces_in, slot_idx, 0, keepdims=False),
            buffer,
        )
        grad_in, grads_now = lax.cond(active, advance, pass_by, (entry_now, fed_in))
        totals_now = tuple((previous + fresh for previous, fresh in zip(totals_now, grads_now)))
        at_first = active & (section_idx == 0)
        returned_now = jnp.where(
            at_first,
            lax.dynamic_update_index_in_dim(returned_now, grad_in, slot_idx, 0),
            returned_now,
        )
        buffer = from_behind(grad_in, "section", -1)
        return (buffer, returned_now, totals_now)

    start_carry = (jnp.zeros_like(pieces_in[0]), returned, totals)
    unused_buffer, returned, totals = lax.fori_loop(0, pieces + sections - 1, tick_fn, start_carry)
    return (returned.reshape(seed_grads.shape), totals)


def gather_blocks(block, rows_axis):
    sections = lax.axis_size("section")
    whole = lax.all_gather(block, ("section", "dp"), axis=0, tiled=True)
    return whole.reshape((sections, -1) + whole.shape[2:])


def scatter_blocks(total):
    sections = lax.axis_size("section")
    groups = lax.axis_size("dp")
    split = total.reshape((sections * groups, total.shape[1] // groups) + total.shape[2:])
    return lax.psum_scatter(
        split.astype(jnp.bfloat16), ("section", "dp"), scatter_dimension=0, tiled=True
    ).astype(jnp.float32)


def network_forward(values, params):
    kernel, norm_gain, layer_scale, w_in, w_out = params
    stored = []
    for block_idx in range(kernel.shape[0]):
        inputs = values
        values, normed, up_proj = block_forward(
            inputs, kernel[block_idx], norm_gain[block_idx], layer_scale[block_idx],
            w_in[block_idx], w_out[block_idx],
        )
        stored.append((inputs, normed, up_proj))
    return values, stored


def network_backward(stored, grad_now, params, with_weights):
    kernel, norm_gain, layer_scale, w_in, w_out = params
    results = [None] * kernel.shape[0]
    for block_idx in reversed(range(kernel.shape[0])):
        inputs, normed, up_proj = stored[block_idx]
        grad_now, grads_now = block_backward(
            inputs, normed, up_proj, grad_now, kernel[block_idx], norm_gain[block_idx],
            layer_scale[block_idx], w_in[block_idx], w_out[block_idx], with_weights,
        )
        results[block_idx] = grads_now
    return grad_now, results


def per_device_flat(features, init_noise, target, kernel, norm_gain, layer_scale, w_in, w_out):
    sections = lax.axis_size("section")
    section_idx = lax.axis_index("section")
    groups = lax.axis_size("dp")
    factor = 1.0 / math.sqrt(features.shape[0] * features.shape[1] * features.shape[2] * groups)
    own = features.shape[0] // sections

    def mine(whole):
        return lax.dynamic_slice_in_dim(whole, section_idx * own, own, 0)

    features, init_noise, target = mine(features), mine(init_noise), mine(target)
    taps = kernel.shape[-1]
    small = jnp.concatenate([kernel, norm_gain[..., None], layer_scale[..., None]], axis=-1)
    small = lax.all_gather(small, "section", axis=0, tiled=True)
    params = (
        small[..., :taps],
        small[..., taps],
        small[..., taps + 1],
        gather_blocks(w_in, 1),
        gather_blocks(w_out, 1),
    )
    clean_in = (features.astype(jnp.float32) + init_noise).astype(jnp.bfloat16)
    outputs, stored = network_forward(clean_in, params)
    seed_grads = ((outputs.astype(jnp.float32) - target.astype(jnp.float32)) * factor).astype(
        jnp.bfloat16
    )
    slope_in, unused_list = network_backward(stored, seed_grads, params, False)
    slope = slope_in.astype(jnp.float32)
    rms_value = jnp.sqrt(jnp.mean(slope * slope, axis=(1, 2, 3), keepdims=True) + 1e-06)
    delta_step = jnp.clip(init_noise + step_size * jnp.tanh(slope / rms_value), -radius, radius)
    adverse = (features.astype(jnp.float32) + delta_step).astype(jnp.bfloat16)
    outputs_adv, stored_adv = network_forward(adverse, params)
    seed_adv = ((outputs_adv.astype(jnp.float32) - target.astype(jnp.float32)) * factor).astype(
        jnp.bfloat16
    )
    unused_grad, grad_list = network_backward(stored_adv, seed_adv, params, True)
    grad_kern, grad_first, grad_second = (
        jnp.stack([grads[part_idx] for grads in grad_list]) for part_idx in range(3)
    )
    taps = grad_kern.shape[-1]
    width = grad_first.shape[-1]
    pad = (-(width + taps)) % 128
    joined = jnp.concatenate(
        [grad_first, grad_kern, jnp.zeros(grad_kern.shape[:2] + (pad,), grad_kern.dtype)], axis=-1
    )
    joined = scatter_blocks(joined)
    return (joined[..., width : width + taps], joined[..., :width], scatter_blocks(grad_second))


def per_device(features, init_noise, target, kernel, norm_gain, layer_scale, w_in, w_out):
    full_in, full_out = (
        lax.all_gather(w_in, "dp", axis=1, tiled=True),
        lax.all_gather(w_out, "dp", axis=1, tiled=True),
    )
    params = (kernel, norm_gain, layer_scale, full_in, full_out)
    pieces = MICRO // 2
    groups = lax.axis_size("dp")
    factor = 1.0 / math.sqrt(features.shape[0] * features.shape[1] * features.shape[2] * groups)
    clean_in = (features.astype(jnp.float32) + init_noise).astype(jnp.bfloat16)
    outputs, saved = run_forward(clean_in, params, pieces)
    seed_grads = ((outputs.astype(jnp.float32) - target.astype(jnp.float32)) * factor).astype(
        jnp.bfloat16
    )
    slope_in, unused_totals = run_backward(saved, seed_grads, params, pieces, False)
    slope = slope_in.astype(jnp.float32)
    rms_value = jnp.sqrt(jnp.mean(slope * slope, axis=(1, 2, 3), keepdims=True) + 1e-06)
    delta_step = jnp.clip(init_noise + step_size * jnp.tanh(slope / rms_value), -radius, radius)
    adverse = (features.astype(jnp.float32) + delta_step).astype(jnp.bfloat16)
    outputs_adv, saved_adv = run_forward(adverse, params, pieces)
    seed_adv = ((outputs_adv.astype(jnp.float32) - target.astype(jnp.float32)) * factor).astype(
        jnp.bfloat16
    )
    unused_grad, totals = run_backward(saved_adv, seed_adv, params, pieces, True)
    grad_kern, grad_first, grad_second = totals
    summed = (
        lax.psum_scatter(
            grad_kern.astype(jnp.bfloat16), "dp", scatter_dimension=1, tiled=True
        ).astype(jnp.float32),
        lax.psum_scatter(
            grad_first.astype(jnp.bfloat16), "dp", scatter_dimension=1, tiled=True
        ).astype(jnp.float32),
        lax.psum_scatter(
            grad_second.astype(jnp.bfloat16), "dp", scatter_dimension=1, tiled=True
        ).astype(jnp.float32),
    )
    return (summed[0], summed[1], summed[2])


def solution(mesh):
    def chosen(features, *rest):
        if features.shape[0] % mesh.shape["section"] == 0:
            return per_device_flat(features, *rest)
        return per_device(features, *rest)

    placed = (
        P(("group", "dp"), None, None, None),
        P(("group", "dp"), None, None, None),
        P(("group", "dp"), None, None, None),
        P("section", None, None),
        P("section", None),
        P("section", None),
        P("section", "dp", None),
        P("section", "dp", None),
    )
    return jax.shard_map(
        chosen,
        mesh=mesh,
        in_specs=placed,
        out_specs=(
            P(("group", "section"), "dp", None),
            P(("group", "section"), "dp", None),
            P(("group", "section"), "dp", None),
        ),
        check_vma=False,
    )
```

```python
import math

import jax
import jax.numpy as jnp
from jax import lax
from jax.sharding import PartitionSpec as P

MICRO = 4


radius = 0.5
step_size = 0.625


def from_behind(block, axis, distance):
    devices = range(lax.axis_size(axis))
    route = [(i - distance, i) for i in devices if i - distance in devices]
    return lax.ppermute(block, axis, route)


def conv_norm(inputs, kernel, norm_gain):
    extent = inputs.shape[1]
    padded = jnp.pad(inputs, ((0, 0), (3, 3), (3, 3), (0, 0)))
    mixture = jnp.zeros_like(inputs)
    for tap_row in range(7):
        for tap_col in range(7):
            mixture = (
                mixture
                + padded[:, tap_row : tap_row + extent, tap_col : tap_col + extent, :]
                * kernel[:, tap_row * 7 + tap_col]
            )
    centre = mixture - jnp.mean(mixture, axis=-1, keepdims=True)
    spread = jnp.mean(centre * centre, axis=-1, keepdims=True)
    return centre * lax.rsqrt(spread + 1e-06) * norm_gain


def gelu_exact(values):
    return jax.nn.gelu(values, approximate=False)


def block_forward(inputs, kernel, norm_gain, layer_scale, w_in, w_out):
    widened = inputs.astype(jnp.float32)
    normed = conv_norm(widened, kernel, norm_gain).astype(jnp.bfloat16)
    channels = inputs.shape[-1]
    up_proj = jnp.dot(normed.reshape(-1, channels), w_in, preferred_element_type=jnp.float32)
    activated = gelu_exact(up_proj).astype(jnp.bfloat16)
    down_proj = jnp.dot(activated, w_out, preferred_element_type=jnp.float32).reshape(inputs.shape)
    result = (widened + layer_scale * down_proj).astype(jnp.bfloat16)
    return (result, normed, up_proj)


def block_backward(
    inputs, normed, up_proj, grad_out, kernel, norm_gain, layer_scale, w_in, w_out, with_weights
):
    channels = inputs.shape[-1]
    outer_grad = grad_out.astype(jnp.float32)
    grad_down = (layer_scale * outer_grad).astype(jnp.bfloat16).reshape(-1, channels)
    grad_act = jnp.dot(grad_down, w_out.T, preferred_element_type=jnp.float32)
    unused_value, gelu_back = jax.vjp(gelu_exact, up_proj)
    grad_up = gelu_back(grad_act)[0].astype(jnp.bfloat16)
    grad_normed = jnp.dot(grad_up, w_in.T, preferred_element_type=jnp.float32).reshape(inputs.shape)
    unused_norm, norm_back = jax.vjp(conv_norm, inputs.astype(jnp.float32), kernel, norm_gain)
    grad_inputs, grad_kern, unused_gain = norm_back(grad_normed)
    grad_in = (outer_grad + grad_inputs).astype(jnp.bfloat16)
    if not with_weights:
        return (grad_in, ())
    activated = gelu_exact(up_proj).astype(jnp.bfloat16)
    grad_first = jnp.dot(
        normed.reshape(-1, channels).T, grad_up, preferred_element_type=jnp.float32
    )
    grad_second = jnp.dot(activated.T, grad_down, preferred_element_type=jnp.float32)
    return (grad_in, (grad_kern, grad_first, grad_second))


def section_forward(values, params):
    kernel, norm_gain, layer_scale, w_in, w_out = params
    inputs_list, normed_list, up_list = ([], [], [])
    inputs_list.append(values)
    values, normed, up_proj = block_forward(
        values, kernel[0], norm_gain[0], layer_scale[0], w_in[0], w_out[0]
    )
    normed_list.append(normed)
    up_list.append(up_proj)
    return (values, (jnp.stack(inputs_list), jnp.stack(normed_list), jnp.stack(up_list)))


def section_backward(entry_now, grad_now, params, with_weights):
    kernel, norm_gain, layer_scale, w_in, w_out = params
    inputs_all, normed_all, up_all = entry_now
    results = []
    for layer_idx in reversed(range(kernel.shape[0])):
        grad_now, grads_now = block_backward(
            inputs_all[layer_idx],
            normed_all[layer_idx],
            up_all[layer_idx],
            grad_now,
            kernel[layer_idx],
            norm_gain[layer_idx],
            layer_scale[layer_idx],
            w_in[layer_idx],
            w_out[layer_idx],
            with_weights,
        )
        results.insert(0, grads_now)
    if not with_weights:
        return (grad_now, ())
    return (
        grad_now,
        tuple((jnp.stack([member[part_idx] for member in results]) for part_idx in range(3))),
    )


def run_forward(inputs, params, pieces):
    sections = lax.axis_size("section")
    section_idx = lax.axis_index("section")
    kernel, norm_gain, layer_scale, w_in, w_out = params
    depth = kernel.shape[0]
    per_piece = inputs.shape[0] // pieces
    pieces_in = inputs.reshape((pieces, per_piece) + inputs.shape[1:])
    rows_piece = per_piece * inputs.shape[1] * inputs.shape[2]
    saved = (
        jnp.zeros((pieces, depth) + pieces_in.shape[1:], jnp.bfloat16),
        jnp.zeros((pieces, depth) + pieces_in.shape[1:], jnp.bfloat16),
        jnp.zeros((pieces, depth, rows_piece, w_in.shape[-1]), jnp.float32),
    )
    outputs = jnp.zeros_like(pieces_in)

    def advance(values):
        return section_forward(values, params)

    def pass_by(values):
        return (values, tuple((jnp.zeros(member.shape[1:], member.dtype) for member in saved)))

    def tick_fn(tick_idx, carry_in):
        buffer, saved_now, outputs_now = carry_in
        slot_raw = tick_idx - section_idx
        active = (slot_raw >= 0) & (slot_raw < pieces)
        slot_idx = jnp.clip(slot_raw, 0, pieces - 1)
        fed_in = jnp.where(
            section_idx == 0,
            lax.dynamic_index_in_dim(pieces_in, slot_idx, 0, keepdims=False),
            buffer,
        )
        result, entry_now = lax.cond(active, advance, pass_by, fed_in)
        saved_now = tuple(
            (
                jnp.where(
                    active, lax.dynamic_update_index_in_dim(previous, fresh, slot_idx, 0), previous
                )
                for previous, fresh in zip(saved_now, entry_now)
            )
        )
        at_end = active & (section_idx == sections - 1)
        outputs_now = jnp.where(
            at_end, lax.dynamic_update_index_in_dim(outputs_now, result, slot_idx, 0), outputs_now
        )
        buffer = from_behind(result, "section", 1)
        return (buffer, saved_now, outputs_now)

    start_carry = (jnp.zeros_like(pieces_in[0]), saved, outputs)
    unused_buffer, saved, outputs = lax.fori_loop(0, pieces + sections - 1, tick_fn, start_carry)
    return (outputs.reshape(inputs.shape), saved)


def run_backward(saved, seed_grads, params, pieces, with_weights):
    sections = lax.axis_size("section")
    section_idx = lax.axis_index("section")
    kernel, norm_gain, layer_scale, w_in, w_out = params
    per_piece = seed_grads.shape[0] // pieces
    pieces_in = seed_grads.reshape((pieces, per_piece) + seed_grads.shape[1:])
    returned = jnp.zeros_like(pieces_in)
    if with_weights:
        totals = (
            jnp.zeros(kernel.shape, jnp.float32),
            jnp.zeros(w_in.shape, jnp.float32),
            jnp.zeros(w_out.shape, jnp.float32),
        )
    else:
        totals = ()

    def advance(operands):
        return section_backward(operands[0], operands[1], params, with_weights)

    def pass_by(operands):
        return (operands[1], tuple((jnp.zeros_like(member) for member in totals)))

    def tick_fn(tick_idx, carry_in):
        buffer, returned_now, totals_now = carry_in
        slot_raw = tick_idx - (sections - 1 - section_idx)
        active = (slot_raw >= 0) & (slot_raw < pieces)
        slot_idx = jnp.clip(slot_raw, 0, pieces - 1)
        entry_now = tuple(
            (lax.dynamic_index_in_dim(member, slot_idx, 0, keepdims=False) for member in saved)
        )
        fed_in = jnp.where(
            section_idx == sections - 1,
            lax.dynamic_index_in_dim(pieces_in, slot_idx, 0, keepdims=False),
            buffer,
        )
        grad_in, grads_now = lax.cond(active, advance, pass_by, (entry_now, fed_in))
        totals_now = tuple((previous + fresh for previous, fresh in zip(totals_now, grads_now)))
        at_first = active & (section_idx == 0)
        returned_now = jnp.where(
            at_first,
            lax.dynamic_update_index_in_dim(returned_now, grad_in, slot_idx, 0),
            returned_now,
        )
        buffer = from_behind(grad_in, "section", -1)
        return (buffer, returned_now, totals_now)

    start_carry = (jnp.zeros_like(pieces_in[0]), returned, totals)
    unused_buffer, returned, totals = lax.fori_loop(0, pieces + sections - 1, tick_fn, start_carry)
    return (returned.reshape(seed_grads.shape), totals)


def gather_blocks(block, rows_axis):
    sections = lax.axis_size("section")
    whole = lax.all_gather(block, ("section", "dp"), axis=0, tiled=True)
    return whole.reshape((sections, -1) + whole.shape[2:])


def scatter_blocks(total):
    sections = lax.axis_size("section")
    groups = lax.axis_size("dp")
    split = total.reshape((sections * groups, total.shape[1] // groups) + total.shape[2:])
    return lax.psum_scatter(
        split.astype(jnp.bfloat16), ("section", "dp"), scatter_dimension=0, tiled=True
    ).astype(jnp.float32)


def network_forward(values, params):
    kernel, norm_gain, layer_scale, w_in, w_out = params
    stored = []
    for block_idx in range(kernel.shape[0]):
        inputs = values
        values, normed, up_proj = block_forward(
            inputs, kernel[block_idx], norm_gain[block_idx], layer_scale[block_idx],
            w_in[block_idx], w_out[block_idx],
        )
        stored.append((inputs, normed, up_proj))
    return values, stored


def network_backward(stored, grad_now, params, with_weights):
    kernel, norm_gain, layer_scale, w_in, w_out = params
    results = [None] * kernel.shape[0]
    for block_idx in reversed(range(kernel.shape[0])):
        inputs, normed, up_proj = stored[block_idx]
        grad_now, grads_now = block_backward(
            inputs, normed, up_proj, grad_now, kernel[block_idx], norm_gain[block_idx],
            layer_scale[block_idx], w_in[block_idx], w_out[block_idx], with_weights,
        )
        results[block_idx] = grads_now
    return grad_now, results


def block_backward_lean(inputs, up_proj, grad_out, kernel, norm_gain, layer_scale, w_in, w_out):
    channels = inputs.shape[-1]
    outer_grad = grad_out.astype(jnp.float32)
    grad_down = (layer_scale * outer_grad).astype(jnp.bfloat16).reshape(-1, channels)
    grad_act = jnp.dot(grad_down, w_out.T, preferred_element_type=jnp.float32)
    unused_value, gelu_back = jax.vjp(gelu_exact, up_proj)
    grad_up = gelu_back(grad_act)[0].astype(jnp.bfloat16)
    grad_normed = jnp.dot(grad_up, w_in.T, preferred_element_type=jnp.float32).reshape(inputs.shape)
    unused_norm, norm_back = jax.vjp(conv_norm, inputs.astype(jnp.float32), kernel, norm_gain)
    grad_inputs, grad_kern, unused_gain = norm_back(grad_normed)
    grad_in = (outer_grad + grad_inputs).astype(jnp.bfloat16)
    return grad_in, grad_kern, grad_down


def owner_weight_grads(normed_all, down_all, w_in, w_out):
    groups = lax.axis_size("dp")
    dp_idx = lax.axis_index("dp")
    rows_in = w_in.shape[0] // groups
    rows_out = w_out.shape[0] // groups
    up_proj = jnp.dot(normed_all, w_in, preferred_element_type=jnp.float32)
    grad_act = jnp.dot(down_all, w_out.T, preferred_element_type=jnp.float32)
    unused_value, gelu_back = jax.vjp(gelu_exact, up_proj)
    grad_up = gelu_back(grad_act)[0].astype(jnp.bfloat16)
    own_normed = lax.dynamic_slice_in_dim(normed_all, dp_idx * rows_in, rows_in, 1)
    grad_first = jnp.dot(own_normed.T, grad_up, preferred_element_type=jnp.float32)
    own_up = lax.dynamic_slice_in_dim(up_proj, dp_idx * rows_out, rows_out, 1)
    activated = gelu_exact(own_up).astype(jnp.bfloat16)
    grad_second = jnp.dot(activated.T, down_all, preferred_element_type=jnp.float32)
    return grad_first, grad_second


def adverse_backward(stored, grad_now, params):
    kernel, norm_gain, layer_scale, w_in, w_out = params
    sections = lax.axis_size("section")
    section_idx = lax.axis_index("section")
    depth = kernel.shape[0]
    kerns, payload = [None] * depth, [None] * depth
    for block_idx in reversed(range(depth)):
        inputs, normed, up_proj = stored[block_idx]
        grad_now, grad_kern, grad_down = block_backward_lean(
            inputs, up_proj, grad_now, kernel[block_idx], norm_gain[block_idx],
            layer_scale[block_idx], w_in[block_idx], w_out[block_idx],
        )
        kerns[block_idx] = grad_kern
        payload[block_idx] = jnp.stack([normed.reshape(grad_down.shape), grad_down])
    grad_kern = scatter_blocks(jnp.stack(kerns))
    per_section = depth // sections
    sent = jnp.stack(payload).reshape((sections, per_section) + payload[0].shape)
    sent = lax.all_to_all(sent, "section", 0, 0, tiled=True)
    sent = lax.all_gather(sent, "dp", axis=0, tiled=True)
    firsts, seconds = [], []
    for local_idx in range(per_section):
        block_idx = section_idx * per_section + local_idx
        mine = sent[:, local_idx]
        normed_all = mine[:, 0].reshape(-1, mine.shape[-1])
        down_all = mine[:, 1].reshape(-1, mine.shape[-1])
        first, second = owner_weight_grads(
            normed_all, down_all,
            lax.dynamic_index_in_dim(w_in, block_idx, 0, keepdims=False),
            lax.dynamic_index_in_dim(w_out, block_idx, 0, keepdims=False),
        )
        firsts.append(first)
        seconds.append(second)
    return grad_kern, jnp.stack(firsts), jnp.stack(seconds)


def per_device_flat(features, init_noise, target, kernel, norm_gain, layer_scale, w_in, w_out):
    sections = lax.axis_size("section")
    section_idx = lax.axis_index("section")
    groups = lax.axis_size("dp")
    factor = 1.0 / math.sqrt(features.shape[0] * features.shape[1] * features.shape[2] * groups)
    own = features.shape[0] // sections

    def mine(whole):
        return lax.dynamic_slice_in_dim(whole, section_idx * own, own, 0)

    features, init_noise, target = mine(features), mine(init_noise), mine(target)
    taps = kernel.shape[-1]
    small = jnp.concatenate([kernel, norm_gain[..., None], layer_scale[..., None]], axis=-1)
    small = lax.all_gather(small, "section", axis=0, tiled=True)
    params = (
        small[..., :taps],
        small[..., taps],
        small[..., taps + 1],
        gather_blocks(w_in, 1),
        gather_blocks(w_out, 1),
    )
    clean_in = (features.astype(jnp.float32) + init_noise).astype(jnp.bfloat16)
    outputs, stored = network_forward(clean_in, params)
    seed_grads = ((outputs.astype(jnp.float32) - target.astype(jnp.float32)) * factor).astype(
        jnp.bfloat16
    )
    slope_in, unused_list = network_backward(stored, seed_grads, params, False)
    slope = slope_in.astype(jnp.float32)
    rms_value = jnp.sqrt(jnp.mean(slope * slope, axis=(1, 2, 3), keepdims=True) + 1e-06)
    delta_step = jnp.clip(init_noise + step_size * jnp.tanh(slope / rms_value), -radius, radius)
    adverse = (features.astype(jnp.float32) + delta_step).astype(jnp.bfloat16)
    outputs_adv, stored_adv = network_forward(adverse, params)
    seed_adv = ((outputs_adv.astype(jnp.float32) - target.astype(jnp.float32)) * factor).astype(
        jnp.bfloat16
    )
    return adverse_backward(stored_adv, seed_adv, params)


def per_device(features, init_noise, target, kernel, norm_gain, layer_scale, w_in, w_out):
    full_in, full_out = (
        lax.all_gather(w_in, "dp", axis=1, tiled=True),
        lax.all_gather(w_out, "dp", axis=1, tiled=True),
    )
    params = (kernel, norm_gain, layer_scale, full_in, full_out)
    pieces = MICRO // 2
    groups = lax.axis_size("dp")
    factor = 1.0 / math.sqrt(features.shape[0] * features.shape[1] * features.shape[2] * groups)
    clean_in = (features.astype(jnp.float32) + init_noise).astype(jnp.bfloat16)
    outputs, saved = run_forward(clean_in, params, pieces)
    seed_grads = ((outputs.astype(jnp.float32) - target.astype(jnp.float32)) * factor).astype(
        jnp.bfloat16
    )
    slope_in, unused_totals = run_backward(saved, seed_grads, params, pieces, False)
    slope = slope_in.astype(jnp.float32)
    rms_value = jnp.sqrt(jnp.mean(slope * slope, axis=(1, 2, 3), keepdims=True) + 1e-06)
    delta_step = jnp.clip(init_noise + step_size * jnp.tanh(slope / rms_value), -radius, radius)
    adverse = (features.astype(jnp.float32) + delta_step).astype(jnp.bfloat16)
    outputs_adv, saved_adv = run_forward(adverse, params, pieces)
    seed_adv = ((outputs_adv.astype(jnp.float32) - target.astype(jnp.float32)) * factor).astype(
        jnp.bfloat16
    )
    unused_grad, totals = run_backward(saved_adv, seed_adv, params, pieces, True)
    grad_kern, grad_first, grad_second = totals
    summed = (
        lax.psum_scatter(
            grad_kern.astype(jnp.bfloat16), "dp", scatter_dimension=1, tiled=True
        ).astype(jnp.float32),
        lax.psum_scatter(
            grad_first.astype(jnp.bfloat16), "dp", scatter_dimension=1, tiled=True
        ).astype(jnp.float32),
        lax.psum_scatter(
            grad_second.astype(jnp.bfloat16), "dp", scatter_dimension=1, tiled=True
        ).astype(jnp.float32),
    )
    return (summed[0], summed[1], summed[2])


def solution(mesh):
    def chosen(features, *rest):
        if features.shape[0] % mesh.shape["section"] == 0:
            return per_device_flat(features, *rest)
        return per_device(features, *rest)

    placed = (
        P(("group", "dp"), None, None, None),
        P(("group", "dp"), None, None, None),
        P(("group", "dp"), None, None, None),
        P("section", None, None),
        P("section", None),
        P("section", None),
        P("section", "dp", None),
        P("section", "dp", None),
    )
    return jax.shard_map(
        chosen,
        mesh=mesh,
        in_specs=placed,
        out_specs=(
            P(("group", "section"), "dp", None),
            P(("group", "section"), "dp", None),
            P(("group", "section"), "dp", None),
        ),
        check_vma=False,
    )
```

```python
import math

import jax
import jax.numpy as jnp
from jax import lax
from jax.sharding import PartitionSpec as P

MICRO = 4


radius = 0.5
step_size = 0.625


def from_behind(block, axis, distance):
    devices = range(lax.axis_size(axis))
    route = [(i - distance, i) for i in devices if i - distance in devices]
    return lax.ppermute(block, axis, route)


def conv_norm(inputs, kernel, norm_gain):
    extent = inputs.shape[1]
    padded = jnp.pad(inputs, ((0, 0), (3, 3), (3, 3), (0, 0)))
    mixture = jnp.zeros_like(inputs)
    for tap_row in range(7):
        for tap_col in range(7):
            mixture = (
                mixture
                + padded[:, tap_row : tap_row + extent, tap_col : tap_col + extent, :]
                * kernel[:, tap_row * 7 + tap_col]
            )
    centre = mixture - jnp.mean(mixture, axis=-1, keepdims=True)
    spread = jnp.mean(centre * centre, axis=-1, keepdims=True)
    return centre * lax.rsqrt(spread + 1e-06) * norm_gain


def gelu_exact(values):
    return jax.nn.gelu(values, approximate=False)


def block_forward(inputs, kernel, norm_gain, layer_scale, w_in, w_out):
    widened = inputs.astype(jnp.float32)
    normed = conv_norm(widened, kernel, norm_gain).astype(jnp.bfloat16)
    channels = inputs.shape[-1]
    up_proj = jnp.dot(normed.reshape(-1, channels), w_in, preferred_element_type=jnp.float32)
    activated = gelu_exact(up_proj).astype(jnp.bfloat16)
    down_proj = jnp.dot(activated, w_out, preferred_element_type=jnp.float32).reshape(inputs.shape)
    result = (widened + layer_scale * down_proj).astype(jnp.bfloat16)
    return (result, normed, up_proj)


def block_backward(
    inputs, normed, up_proj, grad_out, kernel, norm_gain, layer_scale, w_in, w_out, with_weights
):
    channels = inputs.shape[-1]
    outer_grad = grad_out.astype(jnp.float32)
    grad_down = (layer_scale * outer_grad).astype(jnp.bfloat16).reshape(-1, channels)
    grad_act = jnp.dot(grad_down, w_out.T, preferred_element_type=jnp.float32)
    unused_value, gelu_back = jax.vjp(gelu_exact, up_proj)
    grad_up = gelu_back(grad_act)[0].astype(jnp.bfloat16)
    grad_normed = jnp.dot(grad_up, w_in.T, preferred_element_type=jnp.float32).reshape(inputs.shape)
    unused_norm, norm_back = jax.vjp(conv_norm, inputs.astype(jnp.float32), kernel, norm_gain)
    grad_inputs, grad_kern, unused_gain = norm_back(grad_normed)
    grad_in = (outer_grad + grad_inputs).astype(jnp.bfloat16)
    if not with_weights:
        return (grad_in, ())
    activated = gelu_exact(up_proj).astype(jnp.bfloat16)
    grad_first = jnp.dot(
        normed.reshape(-1, channels).T, grad_up, preferred_element_type=jnp.float32
    )
    grad_second = jnp.dot(activated.T, grad_down, preferred_element_type=jnp.float32)
    return (grad_in, (grad_kern, grad_first, grad_second))


def section_forward(values, params):
    kernel, norm_gain, layer_scale, w_in, w_out = params
    inputs_list, normed_list, up_list = ([], [], [])
    inputs_list.append(values)
    values, normed, up_proj = block_forward(
        values, kernel[0], norm_gain[0], layer_scale[0], w_in[0], w_out[0]
    )
    normed_list.append(normed)
    up_list.append(up_proj)
    return (values, (jnp.stack(inputs_list), jnp.stack(normed_list), jnp.stack(up_list)))


def section_backward(entry_now, grad_now, params, with_weights):
    kernel, norm_gain, layer_scale, w_in, w_out = params
    inputs_all, normed_all, up_all = entry_now
    results = []
    for layer_idx in reversed(range(kernel.shape[0])):
        grad_now, grads_now = block_backward(
            inputs_all[layer_idx],
            normed_all[layer_idx],
            up_all[layer_idx],
            grad_now,
            kernel[layer_idx],
            norm_gain[layer_idx],
            layer_scale[layer_idx],
            w_in[layer_idx],
            w_out[layer_idx],
            with_weights,
        )
        results.insert(0, grads_now)
    if not with_weights:
        return (grad_now, ())
    return (
        grad_now,
        tuple((jnp.stack([member[part_idx] for member in results]) for part_idx in range(3))),
    )


def run_forward(inputs, params, pieces):
    sections = lax.axis_size("section")
    section_idx = lax.axis_index("section")
    kernel, norm_gain, layer_scale, w_in, w_out = params
    depth = kernel.shape[0]
    per_piece = inputs.shape[0] // pieces
    pieces_in = inputs.reshape((pieces, per_piece) + inputs.shape[1:])
    rows_piece = per_piece * inputs.shape[1] * inputs.shape[2]
    saved = (
        jnp.zeros((pieces, depth) + pieces_in.shape[1:], jnp.bfloat16),
        jnp.zeros((pieces, depth) + pieces_in.shape[1:], jnp.bfloat16),
        jnp.zeros((pieces, depth, rows_piece, w_in.shape[-1]), jnp.float32),
    )
    outputs = jnp.zeros_like(pieces_in)

    def advance(values):
        return section_forward(values, params)

    def pass_by(values):
        return (values, tuple((jnp.zeros(member.shape[1:], member.dtype) for member in saved)))

    def tick_fn(tick_idx, carry_in):
        buffer, saved_now, outputs_now = carry_in
        slot_raw = tick_idx - section_idx
        active = (slot_raw >= 0) & (slot_raw < pieces)
        slot_idx = jnp.clip(slot_raw, 0, pieces - 1)
        fed_in = jnp.where(
            section_idx == 0,
            lax.dynamic_index_in_dim(pieces_in, slot_idx, 0, keepdims=False),
            buffer,
        )
        result, entry_now = lax.cond(active, advance, pass_by, fed_in)
        saved_now = tuple(
            (
                jnp.where(
                    active, lax.dynamic_update_index_in_dim(previous, fresh, slot_idx, 0), previous
                )
                for previous, fresh in zip(saved_now, entry_now)
            )
        )
        at_end = active & (section_idx == sections - 1)
        outputs_now = jnp.where(
            at_end, lax.dynamic_update_index_in_dim(outputs_now, result, slot_idx, 0), outputs_now
        )
        buffer = from_behind(result, "section", 1)
        return (buffer, saved_now, outputs_now)

    start_carry = (jnp.zeros_like(pieces_in[0]), saved, outputs)
    unused_buffer, saved, outputs = lax.fori_loop(0, pieces + sections - 1, tick_fn, start_carry)
    return (outputs.reshape(inputs.shape), saved)


def run_backward(saved, seed_grads, params, pieces, with_weights):
    sections = lax.axis_size("section")
    section_idx = lax.axis_index("section")
    kernel, norm_gain, layer_scale, w_in, w_out = params
    per_piece = seed_grads.shape[0] // pieces
    pieces_in = seed_grads.reshape((pieces, per_piece) + seed_grads.shape[1:])
    returned = jnp.zeros_like(pieces_in)
    if with_weights:
        totals = (
            jnp.zeros(kernel.shape, jnp.float32),
            jnp.zeros(w_in.shape, jnp.float32),
            jnp.zeros(w_out.shape, jnp.float32),
        )
    else:
        totals = ()

    def advance(operands):
        return section_backward(operands[0], operands[1], params, with_weights)

    def pass_by(operands):
        return (operands[1], tuple((jnp.zeros_like(member) for member in totals)))

    def tick_fn(tick_idx, carry_in):
        buffer, returned_now, totals_now = carry_in
        slot_raw = tick_idx - (sections - 1 - section_idx)
        active = (slot_raw >= 0) & (slot_raw < pieces)
        slot_idx = jnp.clip(slot_raw, 0, pieces - 1)
        entry_now = tuple(
            (lax.dynamic_index_in_dim(member, slot_idx, 0, keepdims=False) for member in saved)
        )
        fed_in = jnp.where(
            section_idx == sections - 1,
            lax.dynamic_index_in_dim(pieces_in, slot_idx, 0, keepdims=False),
            buffer,
        )
        grad_in, grads_now = lax.cond(active, advance, pass_by, (entry_now, fed_in))
        totals_now = tuple((previous + fresh for previous, fresh in zip(totals_now, grads_now)))
        at_first = active & (section_idx == 0)
        returned_now = jnp.where(
            at_first,
            lax.dynamic_update_index_in_dim(returned_now, grad_in, slot_idx, 0),
            returned_now,
        )
        buffer = from_behind(grad_in, "section", -1)
        return (buffer, returned_now, totals_now)

    start_carry = (jnp.zeros_like(pieces_in[0]), returned, totals)
    unused_buffer, returned, totals = lax.fori_loop(0, pieces + sections - 1, tick_fn, start_carry)
    return (returned.reshape(seed_grads.shape), totals)


def gather_blocks(block, rows_axis):
    sections = lax.axis_size("section")
    whole = lax.all_gather(block, ("section", "dp"), axis=0, tiled=True)
    return whole.reshape((sections, -1) + whole.shape[2:])


def scatter_blocks(total):
    sections = lax.axis_size("section")
    groups = lax.axis_size("dp")
    split = total.reshape((sections * groups, total.shape[1] // groups) + total.shape[2:])
    return lax.psum_scatter(
        split.astype(jnp.bfloat16), ("section", "dp"), scatter_dimension=0, tiled=True
    ).astype(jnp.float32)


SQRT_HALF = math.sqrt(0.5)
INV_SQRT_2PI = 1.0 / math.sqrt(2.0 * math.pi)


def block_forward_kept(inputs, kernel, norm_gain, layer_scale, w_in, w_out):
    widened = inputs.astype(jnp.float32)
    normed = conv_norm(widened, kernel, norm_gain).astype(jnp.bfloat16)
    channels = inputs.shape[-1]
    up_proj = jnp.dot(normed.reshape(-1, channels), w_in, preferred_element_type=jnp.float32)
    tail = lax.erfc(-up_proj * SQRT_HALF)
    activated = (0.5 * up_proj * tail).astype(jnp.bfloat16)
    down_proj = jnp.dot(activated, w_out, preferred_element_type=jnp.float32).reshape(inputs.shape)
    result = (widened + layer_scale * down_proj).astype(jnp.bfloat16)
    return result, (inputs, normed, up_proj, tail, activated)


def block_backward_kept(kept, grad_out, kernel, norm_gain, layer_scale, w_in, w_out, with_weights):
    inputs, normed, up_proj, tail, activated = kept
    channels = inputs.shape[-1]
    outer_grad = grad_out.astype(jnp.float32)
    grad_down = (layer_scale * outer_grad).astype(jnp.bfloat16).reshape(-1, channels)
    grad_act = jnp.dot(grad_down, w_out.T, preferred_element_type=jnp.float32)
    slope_gelu = 0.5 * tail + up_proj * jnp.exp(-0.5 * up_proj * up_proj) * INV_SQRT_2PI
    grad_up = (grad_act * slope_gelu).astype(jnp.bfloat16)
    grad_normed = jnp.dot(grad_up, w_in.T, preferred_element_type=jnp.float32).reshape(inputs.shape)
    unused_norm, norm_back = jax.vjp(conv_norm, inputs.astype(jnp.float32), kernel, norm_gain)
    grad_inputs, grad_kern, unused_gain = norm_back(grad_normed)
    grad_in = (outer_grad + grad_inputs).astype(jnp.bfloat16)
    if not with_weights:
        return (grad_in, ())
    grad_first = jnp.dot(
        normed.reshape(-1, channels).T, grad_up, preferred_element_type=jnp.float32
    )
    grad_second = jnp.dot(activated.T, grad_down, preferred_element_type=jnp.float32)
    return (grad_in, (grad_kern, grad_first, grad_second))


def network_forward(values, params):
    kernel, norm_gain, layer_scale, w_in, w_out = params
    stored = []
    for block_idx in range(kernel.shape[0]):
        values, kept = block_forward_kept(
            values, kernel[block_idx], norm_gain[block_idx], layer_scale[block_idx],
            w_in[block_idx], w_out[block_idx],
        )
        stored.append(kept)
    return values, stored


def network_backward(stored, grad_now, params, with_weights):
    kernel, norm_gain, layer_scale, w_in, w_out = params
    results = [None] * kernel.shape[0]
    for block_idx in reversed(range(kernel.shape[0])):
        grad_now, grads_now = block_backward_kept(
            stored[block_idx], grad_now, kernel[block_idx], norm_gain[block_idx],
            layer_scale[block_idx], w_in[block_idx], w_out[block_idx], with_weights,
        )
        results[block_idx] = grads_now
    return grad_now, results


def per_device_flat(features, init_noise, target, kernel, norm_gain, layer_scale, w_in, w_out):
    sections = lax.axis_size("section")
    section_idx = lax.axis_index("section")
    groups = lax.axis_size("dp")
    factor = 1.0 / math.sqrt(features.shape[0] * features.shape[1] * features.shape[2] * groups)
    own = features.shape[0] // sections

    def mine(whole):
        return lax.dynamic_slice_in_dim(whole, section_idx * own, own, 0)

    features, init_noise, target = mine(features), mine(init_noise), mine(target)
    taps = kernel.shape[-1]
    small = jnp.concatenate([kernel, norm_gain[..., None], layer_scale[..., None]], axis=-1)
    small = lax.all_gather(small, "section", axis=0, tiled=True)
    params = (
        small[..., :taps],
        small[..., taps],
        small[..., taps + 1],
        gather_blocks(w_in, 1),
        gather_blocks(w_out, 1),
    )
    clean_in = (features.astype(jnp.float32) + init_noise).astype(jnp.bfloat16)
    outputs, stored = network_forward(clean_in, params)
    seed_grads = ((outputs.astype(jnp.float32) - target.astype(jnp.float32)) * factor).astype(
        jnp.bfloat16
    )
    slope_in, unused_list = network_backward(stored, seed_grads, params, False)
    slope = slope_in.astype(jnp.float32)
    rms_value = jnp.sqrt(jnp.mean(slope * slope, axis=(1, 2, 3), keepdims=True) + 1e-06)
    delta_step = jnp.clip(init_noise + step_size * jnp.tanh(slope / rms_value), -radius, radius)
    adverse = (features.astype(jnp.float32) + delta_step).astype(jnp.bfloat16)
    outputs_adv, stored_adv = network_forward(adverse, params)
    seed_adv = ((outputs_adv.astype(jnp.float32) - target.astype(jnp.float32)) * factor).astype(
        jnp.bfloat16
    )
    unused_grad, grad_list = network_backward(stored_adv, seed_adv, params, True)
    grad_kern, grad_first, grad_second = (
        jnp.stack([grads[part_idx] for grads in grad_list]) for part_idx in range(3)
    )
    taps = grad_kern.shape[-1]
    width = grad_first.shape[-1]
    pad = (-(width + taps)) % 128
    joined = jnp.concatenate(
        [grad_first, grad_kern, jnp.zeros(grad_kern.shape[:2] + (pad,), grad_kern.dtype)], axis=-1
    )
    joined = scatter_blocks(joined)
    return (joined[..., width : width + taps], joined[..., :width], scatter_blocks(grad_second))


def per_device(features, init_noise, target, kernel, norm_gain, layer_scale, w_in, w_out):
    full_in, full_out = (
        lax.all_gather(w_in, "dp", axis=1, tiled=True),
        lax.all_gather(w_out, "dp", axis=1, tiled=True),
    )
    params = (kernel, norm_gain, layer_scale, full_in, full_out)
    pieces = MICRO // 2
    groups = lax.axis_size("dp")
    factor = 1.0 / math.sqrt(features.shape[0] * features.shape[1] * features.shape[2] * groups)
    clean_in = (features.astype(jnp.float32) + init_noise).astype(jnp.bfloat16)
    outputs, saved = run_forward(clean_in, params, pieces)
    seed_grads = ((outputs.astype(jnp.float32) - target.astype(jnp.float32)) * factor).astype(
        jnp.bfloat16
    )
    slope_in, unused_totals = run_backward(saved, seed_grads, params, pieces, False)
    slope = slope_in.astype(jnp.float32)
    rms_value = jnp.sqrt(jnp.mean(slope * slope, axis=(1, 2, 3), keepdims=True) + 1e-06)
    delta_step = jnp.clip(init_noise + step_size * jnp.tanh(slope / rms_value), -radius, radius)
    adverse = (features.astype(jnp.float32) + delta_step).astype(jnp.bfloat16)
    outputs_adv, saved_adv = run_forward(adverse, params, pieces)
    seed_adv = ((outputs_adv.astype(jnp.float32) - target.astype(jnp.float32)) * factor).astype(
        jnp.bfloat16
    )
    unused_grad, totals = run_backward(saved_adv, seed_adv, params, pieces, True)
    grad_kern, grad_first, grad_second = totals
    summed = (
        lax.psum_scatter(
            grad_kern.astype(jnp.bfloat16), "dp", scatter_dimension=1, tiled=True
        ).astype(jnp.float32),
        lax.psum_scatter(
            grad_first.astype(jnp.bfloat16), "dp", scatter_dimension=1, tiled=True
        ).astype(jnp.float32),
        lax.psum_scatter(
            grad_second.astype(jnp.bfloat16), "dp", scatter_dimension=1, tiled=True
        ).astype(jnp.float32),
    )
    return (summed[0], summed[1], summed[2])


def solution(mesh):
    def chosen(features, *rest):
        if features.shape[0] % mesh.shape["section"] == 0:
            return per_device_flat(features, *rest)
        return per_device(features, *rest)

    placed = (
        P(("group", "dp"), None, None, None),
        P(("group", "dp"), None, None, None),
        P(("group", "dp"), None, None, None),
        P("section", None, None),
        P("section", None),
        P("section", None),
        P("section", "dp", None),
        P("section", "dp", None),
    )
    return jax.shard_map(
        chosen,
        mesh=mesh,
        in_specs=placed,
        out_specs=(
            P(("group", "section"), "dp", None),
            P(("group", "section"), "dp", None),
            P(("group", "section"), "dp", None),
        ),
        check_vma=False,
    )
```

```python
import math

import jax
import jax.numpy as jnp
from jax import lax
from jax.sharding import PartitionSpec as P

MICRO = 4


radius = 0.5
step_size = 0.625


def from_behind(block, axis, distance):
    devices = range(lax.axis_size(axis))
    route = [(i - distance, i) for i in devices if i - distance in devices]
    return lax.ppermute(block, axis, route)


def conv_norm(inputs, kernel, norm_gain):
    extent = inputs.shape[1]
    padded = jnp.pad(inputs, ((0, 0), (3, 3), (3, 3), (0, 0)))
    mixture = jnp.zeros_like(inputs)
    for tap_row in range(7):
        for tap_col in range(7):
            mixture = (
                mixture
                + padded[:, tap_row : tap_row + extent, tap_col : tap_col + extent, :]
                * kernel[:, tap_row * 7 + tap_col]
            )
    centre = mixture - jnp.mean(mixture, axis=-1, keepdims=True)
    spread = jnp.mean(centre * centre, axis=-1, keepdims=True)
    return centre * lax.rsqrt(spread + 1e-06) * norm_gain


def gelu_exact(values):
    return jax.nn.gelu(values, approximate=False)


def block_forward(inputs, kernel, norm_gain, layer_scale, w_in, w_out):
    widened = inputs.astype(jnp.float32)
    normed = conv_norm(widened, kernel, norm_gain).astype(jnp.bfloat16)
    channels = inputs.shape[-1]
    up_proj = jnp.dot(normed.reshape(-1, channels), w_in, preferred_element_type=jnp.float32)
    activated = gelu_exact(up_proj).astype(jnp.bfloat16)
    down_proj = jnp.dot(activated, w_out, preferred_element_type=jnp.float32).reshape(inputs.shape)
    result = (widened + layer_scale * down_proj).astype(jnp.bfloat16)
    return (result, normed, up_proj)


def block_backward(
    inputs, normed, up_proj, grad_out, kernel, norm_gain, layer_scale, w_in, w_out, with_weights
):
    channels = inputs.shape[-1]
    outer_grad = grad_out.astype(jnp.float32)
    grad_down = (layer_scale * outer_grad).astype(jnp.bfloat16).reshape(-1, channels)
    grad_act = jnp.dot(grad_down, w_out.T, preferred_element_type=jnp.float32)
    unused_value, gelu_back = jax.vjp(gelu_exact, up_proj)
    grad_up = gelu_back(grad_act)[0].astype(jnp.bfloat16)
    grad_normed = jnp.dot(grad_up, w_in.T, preferred_element_type=jnp.float32).reshape(inputs.shape)
    unused_norm, norm_back = jax.vjp(conv_norm, inputs.astype(jnp.float32), kernel, norm_gain)
    grad_inputs, grad_kern, unused_gain = norm_back(grad_normed)
    grad_in = (outer_grad + grad_inputs).astype(jnp.bfloat16)
    if not with_weights:
        return (grad_in, ())
    activated = gelu_exact(up_proj).astype(jnp.bfloat16)
    grad_first = jnp.dot(
        normed.reshape(-1, channels).T, grad_up, preferred_element_type=jnp.float32
    )
    grad_second = jnp.dot(activated.T, grad_down, preferred_element_type=jnp.float32)
    return (grad_in, (grad_kern, grad_first, grad_second))


def section_forward(values, params):
    kernel, norm_gain, layer_scale, w_in, w_out = params
    inputs_list, normed_list, up_list = ([], [], [])
    inputs_list.append(values)
    values, normed, up_proj = block_forward(
        values, kernel[0], norm_gain[0], layer_scale[0], w_in[0], w_out[0]
    )
    normed_list.append(normed)
    up_list.append(up_proj)
    return (values, (jnp.stack(inputs_list), jnp.stack(normed_list), jnp.stack(up_list)))


def section_backward(entry_now, grad_now, params, with_weights):
    kernel, norm_gain, layer_scale, w_in, w_out = params
    inputs_all, normed_all, up_all = entry_now
    results = []
    for layer_idx in reversed(range(kernel.shape[0])):
        grad_now, grads_now = block_backward(
            inputs_all[layer_idx],
            normed_all[layer_idx],
            up_all[layer_idx],
            grad_now,
            kernel[layer_idx],
            norm_gain[layer_idx],
            layer_scale[layer_idx],
            w_in[layer_idx],
            w_out[layer_idx],
            with_weights,
        )
        results.insert(0, grads_now)
    if not with_weights:
        return (grad_now, ())
    return (
        grad_now,
        tuple((jnp.stack([member[part_idx] for member in results]) for part_idx in range(3))),
    )


def run_forward(inputs, params, pieces):
    sections = lax.axis_size("section")
    section_idx = lax.axis_index("section")
    kernel, norm_gain, layer_scale, w_in, w_out = params
    depth = kernel.shape[0]
    per_piece = inputs.shape[0] // pieces
    pieces_in = inputs.reshape((pieces, per_piece) + inputs.shape[1:])
    rows_piece = per_piece * inputs.shape[1] * inputs.shape[2]
    saved = (
        jnp.zeros((pieces, depth) + pieces_in.shape[1:], jnp.bfloat16),
        jnp.zeros((pieces, depth) + pieces_in.shape[1:], jnp.bfloat16),
        jnp.zeros((pieces, depth, rows_piece, w_in.shape[-1]), jnp.float32),
    )
    outputs = jnp.zeros_like(pieces_in)

    def advance(values):
        return section_forward(values, params)

    def pass_by(values):
        return (values, tuple((jnp.zeros(member.shape[1:], member.dtype) for member in saved)))

    def tick_fn(tick_idx, carry_in):
        buffer, saved_now, outputs_now = carry_in
        slot_raw = tick_idx - section_idx
        active = (slot_raw >= 0) & (slot_raw < pieces)
        slot_idx = jnp.clip(slot_raw, 0, pieces - 1)
        fed_in = jnp.where(
            section_idx == 0,
            lax.dynamic_index_in_dim(pieces_in, slot_idx, 0, keepdims=False),
            buffer,
        )
        result, entry_now = lax.cond(active, advance, pass_by, fed_in)
        saved_now = tuple(
            (
                jnp.where(
                    active, lax.dynamic_update_index_in_dim(previous, fresh, slot_idx, 0), previous
                )
                for previous, fresh in zip(saved_now, entry_now)
            )
        )
        at_end = active & (section_idx == sections - 1)
        outputs_now = jnp.where(
            at_end, lax.dynamic_update_index_in_dim(outputs_now, result, slot_idx, 0), outputs_now
        )
        buffer = from_behind(result, "section", 1)
        return (buffer, saved_now, outputs_now)

    start_carry = (jnp.zeros_like(pieces_in[0]), saved, outputs)
    unused_buffer, saved, outputs = lax.fori_loop(0, pieces + sections - 1, tick_fn, start_carry)
    return (outputs.reshape(inputs.shape), saved)


def run_backward(saved, seed_grads, params, pieces, with_weights):
    sections = lax.axis_size("section")
    section_idx = lax.axis_index("section")
    kernel, norm_gain, layer_scale, w_in, w_out = params
    per_piece = seed_grads.shape[0] // pieces
    pieces_in = seed_grads.reshape((pieces, per_piece) + seed_grads.shape[1:])
    returned = jnp.zeros_like(pieces_in)
    if with_weights:
        totals = (
            jnp.zeros(kernel.shape, jnp.float32),
            jnp.zeros(w_in.shape, jnp.float32),
            jnp.zeros(w_out.shape, jnp.float32),
        )
    else:
        totals = ()

    def advance(operands):
        return section_backward(operands[0], operands[1], params, with_weights)

    def pass_by(operands):
        return (operands[1], tuple((jnp.zeros_like(member) for member in totals)))

    def tick_fn(tick_idx, carry_in):
        buffer, returned_now, totals_now = carry_in
        slot_raw = tick_idx - (sections - 1 - section_idx)
        active = (slot_raw >= 0) & (slot_raw < pieces)
        slot_idx = jnp.clip(slot_raw, 0, pieces - 1)
        entry_now = tuple(
            (lax.dynamic_index_in_dim(member, slot_idx, 0, keepdims=False) for member in saved)
        )
        fed_in = jnp.where(
            section_idx == sections - 1,
            lax.dynamic_index_in_dim(pieces_in, slot_idx, 0, keepdims=False),
            buffer,
        )
        grad_in, grads_now = lax.cond(active, advance, pass_by, (entry_now, fed_in))
        totals_now = tuple((previous + fresh for previous, fresh in zip(totals_now, grads_now)))
        at_first = active & (section_idx == 0)
        returned_now = jnp.where(
            at_first,
            lax.dynamic_update_index_in_dim(returned_now, grad_in, slot_idx, 0),
            returned_now,
        )
        buffer = from_behind(grad_in, "section", -1)
        return (buffer, returned_now, totals_now)

    start_carry = (jnp.zeros_like(pieces_in[0]), returned, totals)
    unused_buffer, returned, totals = lax.fori_loop(0, pieces + sections - 1, tick_fn, start_carry)
    return (returned.reshape(seed_grads.shape), totals)


def gather_blocks(block, rows_axis):
    sections = lax.axis_size("section")
    whole = lax.all_gather(block, ("section", "dp"), axis=0, tiled=True)
    return whole.reshape((sections, -1) + whole.shape[2:])


def scatter_blocks(total):
    sections = lax.axis_size("section")
    groups = lax.axis_size("dp")
    split = total.reshape((sections * groups, total.shape[1] // groups) + total.shape[2:])
    return lax.psum_scatter(
        split.astype(jnp.bfloat16), ("section", "dp"), scatter_dimension=0, tiled=True
    ).astype(jnp.float32)


SQRT_HALF = math.sqrt(0.5)
INV_SQRT_2PI = 1.0 / math.sqrt(2.0 * math.pi)


def depthwise(inputs, kernel):
    extent = inputs.shape[1]
    padded = jnp.pad(inputs, ((0, 0), (3, 3), (3, 3), (0, 0)))
    mixture = jnp.zeros_like(inputs)
    for tap_row in range(7):
        for tap_col in range(7):
            mixture = (
                mixture
                + padded[:, tap_row : tap_row + extent, tap_col : tap_col + extent, :]
                * kernel[:, tap_row * 7 + tap_col]
            )
    return mixture


def conv_norm_back(inputs, kernel, norm_gain, scaled, inv_spread, grad_normed, with_kernel):
    grad_scaled = grad_normed * norm_gain
    first = jnp.mean(grad_scaled, axis=-1, keepdims=True)
    second = jnp.mean(grad_scaled * scaled, axis=-1, keepdims=True)
    grad_mix = inv_spread * (grad_scaled - first - scaled * second)
    grad_inputs = depthwise(grad_mix, kernel[:, ::-1])
    if not with_kernel:
        return grad_inputs, None
    extent = inputs.shape[1]
    padded = jnp.pad(inputs.astype(jnp.float32), ((0, 0), (3, 3), (3, 3), (0, 0)))
    taps = [
        jnp.sum(
            grad_mix * padded[:, tap_row : tap_row + extent, tap_col : tap_col + extent, :],
            axis=(0, 1, 2),
        )
        for tap_row in range(7)
        for tap_col in range(7)
    ]
    return grad_inputs, jnp.stack(taps, axis=-1)


def block_forward_kept(inputs, kernel, norm_gain, layer_scale, w_in, w_out):
    widened = inputs.astype(jnp.float32)
    mixture = depthwise(widened, kernel)
    centre = mixture - jnp.mean(mixture, axis=-1, keepdims=True)
    spread = jnp.mean(centre * centre, axis=-1, keepdims=True)
    inv_spread = lax.rsqrt(spread + 1e-06)
    scaled = centre * inv_spread
    normed = (scaled * norm_gain).astype(jnp.bfloat16)
    channels = inputs.shape[-1]
    up_proj = jnp.dot(normed.reshape(-1, channels), w_in, preferred_element_type=jnp.float32)
    tail = lax.erfc(-up_proj * SQRT_HALF)
    activated = (0.5 * up_proj * tail).astype(jnp.bfloat16)
    down_proj = jnp.dot(activated, w_out, preferred_element_type=jnp.float32).reshape(inputs.shape)
    result = (widened + layer_scale * down_proj).astype(jnp.bfloat16)
    return result, (inputs, normed, up_proj, tail, activated, scaled, inv_spread)


def block_backward_kept(kept, grad_out, kernel, norm_gain, layer_scale, w_in, w_out, with_weights):
    inputs, normed, up_proj, tail, activated, scaled, inv_spread = kept
    channels = inputs.shape[-1]
    outer_grad = grad_out.astype(jnp.float32)
    grad_down = (layer_scale * outer_grad).astype(jnp.bfloat16).reshape(-1, channels)
    grad_act = jnp.dot(grad_down, w_out.T, preferred_element_type=jnp.float32)
    slope_gelu = 0.5 * tail + up_proj * jnp.exp(-0.5 * up_proj * up_proj) * INV_SQRT_2PI
    grad_up = (grad_act * slope_gelu).astype(jnp.bfloat16)
    grad_normed = jnp.dot(grad_up, w_in.T, preferred_element_type=jnp.float32).reshape(inputs.shape)
    grad_inputs, grad_kern = conv_norm_back(
        inputs, kernel, norm_gain, scaled, inv_spread, grad_normed, with_weights
    )
    grad_in = (outer_grad + grad_inputs).astype(jnp.bfloat16)
    if not with_weights:
        return (grad_in, ())
    grad_first = jnp.dot(
        normed.reshape(-1, channels).T, grad_up, preferred_element_type=jnp.float32
    )
    grad_second = jnp.dot(activated.T, grad_down, preferred_element_type=jnp.float32)
    return (grad_in, (grad_kern, grad_first, grad_second))


def network_forward(values, params):
    kernel, norm_gain, layer_scale, w_in, w_out = params
    stored = []
    for block_idx in range(kernel.shape[0]):
        values, kept = block_forward_kept(
            values, kernel[block_idx], norm_gain[block_idx], layer_scale[block_idx],
            w_in[block_idx], w_out[block_idx],
        )
        stored.append(kept)
    return values, stored


def network_backward(stored, grad_now, params, with_weights):
    kernel, norm_gain, layer_scale, w_in, w_out = params
    results = [None] * kernel.shape[0]
    for block_idx in reversed(range(kernel.shape[0])):
        grad_now, grads_now = block_backward_kept(
            stored[block_idx], grad_now, kernel[block_idx], norm_gain[block_idx],
            layer_scale[block_idx], w_in[block_idx], w_out[block_idx], with_weights,
        )
        results[block_idx] = grads_now
    return grad_now, results


def per_device_flat(features, init_noise, target, kernel, norm_gain, layer_scale, w_in, w_out):
    sections = lax.axis_size("section")
    section_idx = lax.axis_index("section")
    groups = lax.axis_size("dp")
    factor = 1.0 / math.sqrt(features.shape[0] * features.shape[1] * features.shape[2] * groups)
    own = features.shape[0] // sections

    def mine(whole):
        return lax.dynamic_slice_in_dim(whole, section_idx * own, own, 0)

    features, init_noise, target = mine(features), mine(init_noise), mine(target)
    taps = kernel.shape[-1]
    small = jnp.concatenate([kernel, norm_gain[..., None], layer_scale[..., None]], axis=-1)
    small = lax.all_gather(small, "section", axis=0, tiled=True)
    params = (
        small[..., :taps],
        small[..., taps],
        small[..., taps + 1],
        gather_blocks(w_in, 1),
        gather_blocks(w_out, 1),
    )
    clean_in = (features.astype(jnp.float32) + init_noise).astype(jnp.bfloat16)
    outputs, stored = network_forward(clean_in, params)
    seed_grads = ((outputs.astype(jnp.float32) - target.astype(jnp.float32)) * factor).astype(
        jnp.bfloat16
    )
    slope_in, unused_list = network_backward(stored, seed_grads, params, False)
    slope = slope_in.astype(jnp.float32)
    rms_value = jnp.sqrt(jnp.mean(slope * slope, axis=(1, 2, 3), keepdims=True) + 1e-06)
    delta_step = jnp.clip(init_noise + step_size * jnp.tanh(slope / rms_value), -radius, radius)
    adverse = (features.astype(jnp.float32) + delta_step).astype(jnp.bfloat16)
    outputs_adv, stored_adv = network_forward(adverse, params)
    seed_adv = ((outputs_adv.astype(jnp.float32) - target.astype(jnp.float32)) * factor).astype(
        jnp.bfloat16
    )
    unused_grad, grad_list = network_backward(stored_adv, seed_adv, params, True)
    grad_kern, grad_first, grad_second = (
        jnp.stack([grads[part_idx] for grads in grad_list]) for part_idx in range(3)
    )
    taps = grad_kern.shape[-1]
    width = grad_first.shape[-1]
    pad = (-(width + taps)) % 128
    joined = jnp.concatenate(
        [grad_first, grad_kern, jnp.zeros(grad_kern.shape[:2] + (pad,), grad_kern.dtype)], axis=-1
    )
    joined = scatter_blocks(joined)
    return (joined[..., width : width + taps], joined[..., :width], scatter_blocks(grad_second))


def per_device(features, init_noise, target, kernel, norm_gain, layer_scale, w_in, w_out):
    full_in, full_out = (
        lax.all_gather(w_in, "dp", axis=1, tiled=True),
        lax.all_gather(w_out, "dp", axis=1, tiled=True),
    )
    params = (kernel, norm_gain, layer_scale, full_in, full_out)
    pieces = MICRO // 2
    groups = lax.axis_size("dp")
    factor = 1.0 / math.sqrt(features.shape[0] * features.shape[1] * features.shape[2] * groups)
    clean_in = (features.astype(jnp.float32) + init_noise).astype(jnp.bfloat16)
    outputs, saved = run_forward(clean_in, params, pieces)
    seed_grads = ((outputs.astype(jnp.float32) - target.astype(jnp.float32)) * factor).astype(
        jnp.bfloat16
    )
    slope_in, unused_totals = run_backward(saved, seed_grads, params, pieces, False)
    slope = slope_in.astype(jnp.float32)
    rms_value = jnp.sqrt(jnp.mean(slope * slope, axis=(1, 2, 3), keepdims=True) + 1e-06)
    delta_step = jnp.clip(init_noise + step_size * jnp.tanh(slope / rms_value), -radius, radius)
    adverse = (features.astype(jnp.float32) + delta_step).astype(jnp.bfloat16)
    outputs_adv, saved_adv = run_forward(adverse, params, pieces)
    seed_adv = ((outputs_adv.astype(jnp.float32) - target.astype(jnp.float32)) * factor).astype(
        jnp.bfloat16
    )
    unused_grad, totals = run_backward(saved_adv, seed_adv, params, pieces, True)
    grad_kern, grad_first, grad_second = totals
    summed = (
        lax.psum_scatter(
            grad_kern.astype(jnp.bfloat16), "dp", scatter_dimension=1, tiled=True
        ).astype(jnp.float32),
        lax.psum_scatter(
            grad_first.astype(jnp.bfloat16), "dp", scatter_dimension=1, tiled=True
        ).astype(jnp.float32),
        lax.psum_scatter(
            grad_second.astype(jnp.bfloat16), "dp", scatter_dimension=1, tiled=True
        ).astype(jnp.float32),
    )
    return (summed[0], summed[1], summed[2])


def solution(mesh):
    def chosen(features, *rest):
        if features.shape[0] % mesh.shape["section"] == 0:
            return per_device_flat(features, *rest)
        return per_device(features, *rest)

    placed = (
        P(("group", "dp"), None, None, None),
        P(("group", "dp"), None, None, None),
        P(("group", "dp"), None, None, None),
        P("section", None, None),
        P("section", None),
        P("section", None),
        P("section", "dp", None),
        P("section", "dp", None),
    )
    return jax.shard_map(
        chosen,
        mesh=mesh,
        in_specs=placed,
        out_specs=(
            P(("group", "section"), "dp", None),
            P(("group", "section"), "dp", None),
            P(("group", "section"), "dp", None),
        ),
        check_vma=False,
    )
```

```python
import math

import jax
import jax.numpy as jnp
from jax import lax
from jax.sharding import PartitionSpec as P

MICRO = 4


radius = 0.5
step_size = 0.625


def from_behind(block, axis, distance):
    devices = range(lax.axis_size(axis))
    route = [(i - distance, i) for i in devices if i - distance in devices]
    return lax.ppermute(block, axis, route)


def conv_norm(inputs, kernel, norm_gain):
    extent = inputs.shape[1]
    padded = jnp.pad(inputs, ((0, 0), (3, 3), (3, 3), (0, 0)))
    mixture = jnp.zeros_like(inputs)
    for tap_row in range(7):
        for tap_col in range(7):
            mixture = (
                mixture
                + padded[:, tap_row : tap_row + extent, tap_col : tap_col + extent, :]
                * kernel[:, tap_row * 7 + tap_col]
            )
    centre = mixture - jnp.mean(mixture, axis=-1, keepdims=True)
    spread = jnp.mean(centre * centre, axis=-1, keepdims=True)
    return centre * lax.rsqrt(spread + 1e-06) * norm_gain


def gelu_exact(values):
    return jax.nn.gelu(values, approximate=False)


def block_forward(inputs, kernel, norm_gain, layer_scale, w_in, w_out):
    widened = inputs.astype(jnp.float32)
    normed = conv_norm(widened, kernel, norm_gain).astype(jnp.bfloat16)
    channels = inputs.shape[-1]
    up_proj = jnp.dot(normed.reshape(-1, channels), w_in, preferred_element_type=jnp.float32)
    activated = gelu_exact(up_proj).astype(jnp.bfloat16)
    down_proj = jnp.dot(activated, w_out, preferred_element_type=jnp.float32).reshape(inputs.shape)
    result = (widened + layer_scale * down_proj).astype(jnp.bfloat16)
    return (result, normed, up_proj)


def block_backward(
    inputs, normed, up_proj, grad_out, kernel, norm_gain, layer_scale, w_in, w_out, with_weights
):
    channels = inputs.shape[-1]
    outer_grad = grad_out.astype(jnp.float32)
    grad_down = (layer_scale * outer_grad).astype(jnp.bfloat16).reshape(-1, channels)
    grad_act = jnp.dot(grad_down, w_out.T, preferred_element_type=jnp.float32)
    unused_value, gelu_back = jax.vjp(gelu_exact, up_proj)
    grad_up = gelu_back(grad_act)[0].astype(jnp.bfloat16)
    grad_normed = jnp.dot(grad_up, w_in.T, preferred_element_type=jnp.float32).reshape(inputs.shape)
    unused_norm, norm_back = jax.vjp(conv_norm, inputs.astype(jnp.float32), kernel, norm_gain)
    grad_inputs, grad_kern, unused_gain = norm_back(grad_normed)
    grad_in = (outer_grad + grad_inputs).astype(jnp.bfloat16)
    if not with_weights:
        return (grad_in, ())
    activated = gelu_exact(up_proj).astype(jnp.bfloat16)
    grad_first = jnp.dot(
        normed.reshape(-1, channels).T, grad_up, preferred_element_type=jnp.float32
    )
    grad_second = jnp.dot(activated.T, grad_down, preferred_element_type=jnp.float32)
    return (grad_in, (grad_kern, grad_first, grad_second))


def section_forward(values, params):
    kernel, norm_gain, layer_scale, w_in, w_out = params
    inputs_list, normed_list, up_list = ([], [], [])
    inputs_list.append(values)
    values, normed, up_proj = block_forward(
        values, kernel[0], norm_gain[0], layer_scale[0], w_in[0], w_out[0]
    )
    normed_list.append(normed)
    up_list.append(up_proj)
    return (values, (jnp.stack(inputs_list), jnp.stack(normed_list), jnp.stack(up_list)))


def section_backward(entry_now, grad_now, params, with_weights):
    kernel, norm_gain, layer_scale, w_in, w_out = params
    inputs_all, normed_all, up_all = entry_now
    results = []
    for layer_idx in reversed(range(kernel.shape[0])):
        grad_now, grads_now = block_backward(
            inputs_all[layer_idx],
            normed_all[layer_idx],
            up_all[layer_idx],
            grad_now,
            kernel[layer_idx],
            norm_gain[layer_idx],
            layer_scale[layer_idx],
            w_in[layer_idx],
            w_out[layer_idx],
            with_weights,
        )
        results.insert(0, grads_now)
    if not with_weights:
        return (grad_now, ())
    return (
        grad_now,
        tuple((jnp.stack([member[part_idx] for member in results]) for part_idx in range(3))),
    )


def run_forward(inputs, params, pieces):
    sections = lax.axis_size("section")
    section_idx = lax.axis_index("section")
    kernel, norm_gain, layer_scale, w_in, w_out = params
    depth = kernel.shape[0]
    per_piece = inputs.shape[0] // pieces
    pieces_in = inputs.reshape((pieces, per_piece) + inputs.shape[1:])
    rows_piece = per_piece * inputs.shape[1] * inputs.shape[2]
    saved = (
        jnp.zeros((pieces, depth) + pieces_in.shape[1:], jnp.bfloat16),
        jnp.zeros((pieces, depth) + pieces_in.shape[1:], jnp.bfloat16),
        jnp.zeros((pieces, depth, rows_piece, w_in.shape[-1]), jnp.float32),
    )
    outputs = jnp.zeros_like(pieces_in)

    def advance(values):
        return section_forward(values, params)

    def pass_by(values):
        return (values, tuple((jnp.zeros(member.shape[1:], member.dtype) for member in saved)))

    def tick_fn(tick_idx, carry_in):
        buffer, saved_now, outputs_now = carry_in
        slot_raw = tick_idx - section_idx
        active = (slot_raw >= 0) & (slot_raw < pieces)
        slot_idx = jnp.clip(slot_raw, 0, pieces - 1)
        fed_in = jnp.where(
            section_idx == 0,
            lax.dynamic_index_in_dim(pieces_in, slot_idx, 0, keepdims=False),
            buffer,
        )
        result, entry_now = lax.cond(active, advance, pass_by, fed_in)
        saved_now = tuple(
            (
                jnp.where(
                    active, lax.dynamic_update_index_in_dim(previous, fresh, slot_idx, 0), previous
                )
                for previous, fresh in zip(saved_now, entry_now)
            )
        )
        at_end = active & (section_idx == sections - 1)
        outputs_now = jnp.where(
            at_end, lax.dynamic_update_index_in_dim(outputs_now, result, slot_idx, 0), outputs_now
        )
        buffer = from_behind(result, "section", 1)
        return (buffer, saved_now, outputs_now)

    start_carry = (jnp.zeros_like(pieces_in[0]), saved, outputs)
    unused_buffer, saved, outputs = lax.fori_loop(0, pieces + sections - 1, tick_fn, start_carry)
    return (outputs.reshape(inputs.shape), saved)


def run_backward(saved, seed_grads, params, pieces, with_weights):
    sections = lax.axis_size("section")
    section_idx = lax.axis_index("section")
    kernel, norm_gain, layer_scale, w_in, w_out = params
    per_piece = seed_grads.shape[0] // pieces
    pieces_in = seed_grads.reshape((pieces, per_piece) + seed_grads.shape[1:])
    returned = jnp.zeros_like(pieces_in)
    if with_weights:
        totals = (
            jnp.zeros(kernel.shape, jnp.float32),
            jnp.zeros(w_in.shape, jnp.float32),
            jnp.zeros(w_out.shape, jnp.float32),
        )
    else:
        totals = ()

    def advance(operands):
        return section_backward(operands[0], operands[1], params, with_weights)

    def pass_by(operands):
        return (operands[1], tuple((jnp.zeros_like(member) for member in totals)))

    def tick_fn(tick_idx, carry_in):
        buffer, returned_now, totals_now = carry_in
        slot_raw = tick_idx - (sections - 1 - section_idx)
        active = (slot_raw >= 0) & (slot_raw < pieces)
        slot_idx = jnp.clip(slot_raw, 0, pieces - 1)
        entry_now = tuple(
            (lax.dynamic_index_in_dim(member, slot_idx, 0, keepdims=False) for member in saved)
        )
        fed_in = jnp.where(
            section_idx == sections - 1,
            lax.dynamic_index_in_dim(pieces_in, slot_idx, 0, keepdims=False),
            buffer,
        )
        grad_in, grads_now = lax.cond(active, advance, pass_by, (entry_now, fed_in))
        totals_now = tuple((previous + fresh for previous, fresh in zip(totals_now, grads_now)))
        at_first = active & (section_idx == 0)
        returned_now = jnp.where(
            at_first,
            lax.dynamic_update_index_in_dim(returned_now, grad_in, slot_idx, 0),
            returned_now,
        )
        buffer = from_behind(grad_in, "section", -1)
        return (buffer, returned_now, totals_now)

    start_carry = (jnp.zeros_like(pieces_in[0]), returned, totals)
    unused_buffer, returned, totals = lax.fori_loop(0, pieces + sections - 1, tick_fn, start_carry)
    return (returned.reshape(seed_grads.shape), totals)


def gather_blocks(block, rows_axis):
    sections = lax.axis_size("section")
    whole = lax.all_gather(block, ("section", "dp"), axis=0, tiled=True)
    return whole.reshape((sections, -1) + whole.shape[2:])


def scatter_blocks(total):
    sections = lax.axis_size("section")
    groups = lax.axis_size("dp")
    split = total.reshape((sections * groups, total.shape[1] // groups) + total.shape[2:])
    return lax.psum_scatter(
        split.astype(jnp.bfloat16), ("section", "dp"), scatter_dimension=0, tiled=True
    ).astype(jnp.float32)


SQRT_HALF = math.sqrt(0.5)
INV_SQRT_2PI = 1.0 / math.sqrt(2.0 * math.pi)


def block_forward_kept(inputs, kernel, norm_gain, layer_scale, w_in, w_out):
    widened = inputs.astype(jnp.float32)
    normed = conv_norm(widened, kernel, norm_gain).astype(jnp.bfloat16)
    channels = inputs.shape[-1]
    up_proj = jnp.dot(normed.reshape(-1, channels), w_in, preferred_element_type=jnp.float32)
    tail = lax.erfc(-up_proj * SQRT_HALF)
    activated = (0.5 * up_proj * tail).astype(jnp.bfloat16)
    down_proj = jnp.dot(activated, w_out, preferred_element_type=jnp.float32).reshape(inputs.shape)
    result = (widened + layer_scale * down_proj).astype(jnp.bfloat16)
    return result, (inputs, normed, up_proj, tail, activated)


def block_backward_kept(kept, grad_out, kernel, norm_gain, layer_scale, w_in, w_out, with_weights):
    inputs, normed, up_proj, tail, activated = kept
    channels = inputs.shape[-1]
    outer_grad = grad_out.astype(jnp.float32)
    grad_down = (layer_scale * outer_grad).astype(jnp.bfloat16).reshape(-1, channels)
    grad_act = jnp.dot(grad_down, w_out.T, preferred_element_type=jnp.float32)
    slope_gelu = 0.5 * tail + up_proj * jnp.exp(-0.5 * up_proj * up_proj) * INV_SQRT_2PI
    grad_up = (grad_act * slope_gelu).astype(jnp.bfloat16)
    grad_normed = jnp.dot(grad_up, w_in.T, preferred_element_type=jnp.float32).reshape(inputs.shape)
    unused_norm, norm_back = jax.vjp(conv_norm, inputs.astype(jnp.float32), kernel, norm_gain)
    grad_inputs, grad_kern, unused_gain = norm_back(grad_normed)
    grad_in = (outer_grad + grad_inputs).astype(jnp.bfloat16)
    if not with_weights:
        return (grad_in, ())
    grad_first = jnp.dot(
        normed.reshape(-1, channels).T, grad_up, preferred_element_type=jnp.float32
    )
    grad_second = jnp.dot(activated.T, grad_down, preferred_element_type=jnp.float32)
    return (grad_in, (grad_kern, grad_first, grad_second))


def network_forward(values, params):
    kernel, norm_gain, layer_scale, w_in, w_out = params
    stored = []
    for block_idx in range(kernel.shape[0]):
        values, kept = block_forward_kept(
            values, kernel[block_idx], norm_gain[block_idx], layer_scale[block_idx],
            w_in[block_idx], w_out[block_idx],
        )
        stored.append(kept)
    return values, stored


def network_backward(stored, grad_now, params, with_weights):
    kernel, norm_gain, layer_scale, w_in, w_out = params
    results = [None] * kernel.shape[0]
    for block_idx in reversed(range(kernel.shape[0])):
        grad_now, grads_now = block_backward_kept(
            stored[block_idx], grad_now, kernel[block_idx], norm_gain[block_idx],
            layer_scale[block_idx], w_in[block_idx], w_out[block_idx], with_weights,
        )
        results[block_idx] = grads_now
    return grad_now, results


def per_device_flat(features, init_noise, target, kernel, norm_gain, layer_scale, w_in, w_out):
    sections = lax.axis_size("section")
    section_idx = lax.axis_index("section")
    groups = lax.axis_size("dp")
    factor = 1.0 / math.sqrt(features.shape[0] * features.shape[1] * features.shape[2] * groups)
    own = features.shape[0] // sections

    def mine(whole):
        return lax.dynamic_slice_in_dim(whole, section_idx * own, own, 0)

    features, init_noise, target = mine(features), mine(init_noise), mine(target)
    taps = kernel.shape[-1]
    small = jnp.concatenate([kernel, norm_gain[..., None], layer_scale[..., None]], axis=-1)
    small = lax.all_gather(small, "section", axis=0, tiled=True)
    params = (
        small[..., :taps],
        small[..., taps],
        small[..., taps + 1],
        gather_blocks(w_in, 1),
        gather_blocks(w_out, 1),
    )
    clean_in = (features.astype(jnp.float32) + init_noise).astype(jnp.bfloat16)
    outputs, stored = network_forward(clean_in, params)
    seed_grads = ((outputs.astype(jnp.float32) - target.astype(jnp.float32)) * factor).astype(
        jnp.bfloat16
    )
    slope_in, unused_list = network_backward(stored, seed_grads, params, False)
    slope = slope_in.astype(jnp.float32)
    rms_value = jnp.sqrt(jnp.mean(slope * slope, axis=(1, 2, 3), keepdims=True) + 1e-06)
    delta_step = jnp.clip(init_noise + step_size * jnp.tanh(slope / rms_value), -radius, radius)
    adverse = (features.astype(jnp.float32) + delta_step).astype(jnp.bfloat16)
    outputs_adv, stored_adv = network_forward(adverse, params)
    seed_adv = ((outputs_adv.astype(jnp.float32) - target.astype(jnp.float32)) * factor).astype(
        jnp.bfloat16
    )
    unused_grad, grad_list = network_backward(stored_adv, seed_adv, params, True)
    grad_second = jnp.stack([grads[2] for grads in grad_list])
    taps = grad_list[0][0].shape[-1]
    width = grad_list[0][1].shape[-1]
    pad = (-(width + taps)) % 128
    joined = jnp.stack([
        jnp.concatenate(
            [
                grads[1].astype(jnp.bfloat16),
                grads[0].astype(jnp.bfloat16),
                jnp.zeros(grads[0].shape[:1] + (pad,), jnp.bfloat16),
            ],
            axis=-1,
        )
        for grads in grad_list
    ])
    joined = scatter_blocks(joined)
    return (joined[..., width : width + taps], joined[..., :width], scatter_blocks(grad_second))


def per_device(features, init_noise, target, kernel, norm_gain, layer_scale, w_in, w_out):
    full_in, full_out = (
        lax.all_gather(w_in, "dp", axis=1, tiled=True),
        lax.all_gather(w_out, "dp", axis=1, tiled=True),
    )
    params = (kernel, norm_gain, layer_scale, full_in, full_out)
    pieces = MICRO // 2
    groups = lax.axis_size("dp")
    factor = 1.0 / math.sqrt(features.shape[0] * features.shape[1] * features.shape[2] * groups)
    clean_in = (features.astype(jnp.float32) + init_noise).astype(jnp.bfloat16)
    outputs, saved = run_forward(clean_in, params, pieces)
    seed_grads = ((outputs.astype(jnp.float32) - target.astype(jnp.float32)) * factor).astype(
        jnp.bfloat16
    )
    slope_in, unused_totals = run_backward(saved, seed_grads, params, pieces, False)
    slope = slope_in.astype(jnp.float32)
    rms_value = jnp.sqrt(jnp.mean(slope * slope, axis=(1, 2, 3), keepdims=True) + 1e-06)
    delta_step = jnp.clip(init_noise + step_size * jnp.tanh(slope / rms_value), -radius, radius)
    adverse = (features.astype(jnp.float32) + delta_step).astype(jnp.bfloat16)
    outputs_adv, saved_adv = run_forward(adverse, params, pieces)
    seed_adv = ((outputs_adv.astype(jnp.float32) - target.astype(jnp.float32)) * factor).astype(
        jnp.bfloat16
    )
    unused_grad, totals = run_backward(saved_adv, seed_adv, params, pieces, True)
    grad_kern, grad_first, grad_second = totals
    summed = (
        lax.psum_scatter(
            grad_kern.astype(jnp.bfloat16), "dp", scatter_dimension=1, tiled=True
        ).astype(jnp.float32),
        lax.psum_scatter(
            grad_first.astype(jnp.bfloat16), "dp", scatter_dimension=1, tiled=True
        ).astype(jnp.float32),
        lax.psum_scatter(
            grad_second.astype(jnp.bfloat16), "dp", scatter_dimension=1, tiled=True
        ).astype(jnp.float32),
    )
    return (summed[0], summed[1], summed[2])


def solution(mesh):
    def chosen(features, *rest):
        if features.shape[0] % mesh.shape["section"] == 0:
            return per_device_flat(features, *rest)
        return per_device(features, *rest)

    placed = (
        P(("group", "dp"), None, None, None),
        P(("group", "dp"), None, None, None),
        P(("group", "dp"), None, None, None),
        P("section", None, None),
        P("section", None),
        P("section", None),
        P("section", "dp", None),
        P("section", "dp", None),
    )
    return jax.shard_map(
        chosen,
        mesh=mesh,
        in_specs=placed,
        out_specs=(
            P(("group", "section"), "dp", None),
            P(("group", "section"), "dp", None),
            P(("group", "section"), "dp", None),
        ),
        check_vma=False,
    )
```

```python
import math

import jax
import jax.numpy as jnp
from jax import lax
from jax.sharding import PartitionSpec as P

MICRO = 4


radius = 0.5
step_size = 0.625


def from_behind(block, axis, distance):
    devices = range(lax.axis_size(axis))
    route = [(i - distance, i) for i in devices if i - distance in devices]
    return lax.ppermute(block, axis, route)


def conv_norm(inputs, kernel, norm_gain):
    extent = inputs.shape[1]
    padded = jnp.pad(inputs, ((0, 0), (3, 3), (3, 3), (0, 0)))
    mixture = jnp.zeros_like(inputs)
    for tap_row in range(7):
        for tap_col in range(7):
            mixture = (
                mixture
                + padded[:, tap_row : tap_row + extent, tap_col : tap_col + extent, :]
                * kernel[:, tap_row * 7 + tap_col]
            )
    centre = mixture - jnp.mean(mixture, axis=-1, keepdims=True)
    spread = jnp.mean(centre * centre, axis=-1, keepdims=True)
    return centre * lax.rsqrt(spread + 1e-06) * norm_gain


def gelu_exact(values):
    return jax.nn.gelu(values, approximate=False)


def block_forward(inputs, kernel, norm_gain, layer_scale, w_in, w_out):
    widened = inputs.astype(jnp.float32)
    normed = conv_norm(widened, kernel, norm_gain).astype(jnp.bfloat16)
    channels = inputs.shape[-1]
    up_proj = jnp.dot(normed.reshape(-1, channels), w_in, preferred_element_type=jnp.float32)
    activated = gelu_exact(up_proj).astype(jnp.bfloat16)
    down_proj = jnp.dot(activated, w_out, preferred_element_type=jnp.float32).reshape(inputs.shape)
    result = (widened + layer_scale * down_proj).astype(jnp.bfloat16)
    return (result, normed, up_proj)


def block_backward(
    inputs, normed, up_proj, grad_out, kernel, norm_gain, layer_scale, w_in, w_out, with_weights
):
    channels = inputs.shape[-1]
    outer_grad = grad_out.astype(jnp.float32)
    grad_down = (layer_scale * outer_grad).astype(jnp.bfloat16).reshape(-1, channels)
    grad_act = jnp.dot(grad_down, w_out.T, preferred_element_type=jnp.float32)
    unused_value, gelu_back = jax.vjp(gelu_exact, up_proj)
    grad_up = gelu_back(grad_act)[0].astype(jnp.bfloat16)
    grad_normed = jnp.dot(grad_up, w_in.T, preferred_element_type=jnp.float32).reshape(inputs.shape)
    unused_norm, norm_back = jax.vjp(conv_norm, inputs.astype(jnp.float32), kernel, norm_gain)
    grad_inputs, grad_kern, unused_gain = norm_back(grad_normed)
    grad_in = (outer_grad + grad_inputs).astype(jnp.bfloat16)
    if not with_weights:
        return (grad_in, ())
    activated = gelu_exact(up_proj).astype(jnp.bfloat16)
    grad_first = jnp.dot(
        normed.reshape(-1, channels).T, grad_up, preferred_element_type=jnp.float32
    )
    grad_second = jnp.dot(activated.T, grad_down, preferred_element_type=jnp.float32)
    return (grad_in, (grad_kern, grad_first, grad_second))


def section_forward(values, params):
    kernel, norm_gain, layer_scale, w_in, w_out = params
    inputs_list, normed_list, up_list = ([], [], [])
    inputs_list.append(values)
    values, normed, up_proj = block_forward(
        values, kernel[0], norm_gain[0], layer_scale[0], w_in[0], w_out[0]
    )
    normed_list.append(normed)
    up_list.append(up_proj)
    return (values, (jnp.stack(inputs_list), jnp.stack(normed_list), jnp.stack(up_list)))


def section_backward(entry_now, grad_now, params, with_weights):
    kernel, norm_gain, layer_scale, w_in, w_out = params
    inputs_all, normed_all, up_all = entry_now
    results = []
    for layer_idx in reversed(range(kernel.shape[0])):
        grad_now, grads_now = block_backward(
            inputs_all[layer_idx],
            normed_all[layer_idx],
            up_all[layer_idx],
            grad_now,
            kernel[layer_idx],
            norm_gain[layer_idx],
            layer_scale[layer_idx],
            w_in[layer_idx],
            w_out[layer_idx],
            with_weights,
        )
        results.insert(0, grads_now)
    if not with_weights:
        return (grad_now, ())
    return (
        grad_now,
        tuple((jnp.stack([member[part_idx] for member in results]) for part_idx in range(3))),
    )


def run_forward(inputs, params, pieces):
    sections = lax.axis_size("section")
    section_idx = lax.axis_index("section")
    kernel, norm_gain, layer_scale, w_in, w_out = params
    depth = kernel.shape[0]
    per_piece = inputs.shape[0] // pieces
    pieces_in = inputs.reshape((pieces, per_piece) + inputs.shape[1:])
    rows_piece = per_piece * inputs.shape[1] * inputs.shape[2]
    saved = (
        jnp.zeros((pieces, depth) + pieces_in.shape[1:], jnp.bfloat16),
        jnp.zeros((pieces, depth) + pieces_in.shape[1:], jnp.bfloat16),
        jnp.zeros((pieces, depth, rows_piece, w_in.shape[-1]), jnp.float32),
    )
    outputs = jnp.zeros_like(pieces_in)

    def advance(values):
        return section_forward(values, params)

    def pass_by(values):
        return (values, tuple((jnp.zeros(member.shape[1:], member.dtype) for member in saved)))

    def tick_fn(tick_idx, carry_in):
        buffer, saved_now, outputs_now = carry_in
        slot_raw = tick_idx - section_idx
        active = (slot_raw >= 0) & (slot_raw < pieces)
        slot_idx = jnp.clip(slot_raw, 0, pieces - 1)
        fed_in = jnp.where(
            section_idx == 0,
            lax.dynamic_index_in_dim(pieces_in, slot_idx, 0, keepdims=False),
            buffer,
        )
        result, entry_now = lax.cond(active, advance, pass_by, fed_in)
        saved_now = tuple(
            (
                jnp.where(
                    active, lax.dynamic_update_index_in_dim(previous, fresh, slot_idx, 0), previous
                )
                for previous, fresh in zip(saved_now, entry_now)
            )
        )
        at_end = active & (section_idx == sections - 1)
        outputs_now = jnp.where(
            at_end, lax.dynamic_update_index_in_dim(outputs_now, result, slot_idx, 0), outputs_now
        )
        buffer = from_behind(result, "section", 1)
        return (buffer, saved_now, outputs_now)

    start_carry = (jnp.zeros_like(pieces_in[0]), saved, outputs)
    unused_buffer, saved, outputs = lax.fori_loop(0, pieces + sections - 1, tick_fn, start_carry)
    return (outputs.reshape(inputs.shape), saved)


def run_backward(saved, seed_grads, params, pieces, with_weights):
    sections = lax.axis_size("section")
    section_idx = lax.axis_index("section")
    kernel, norm_gain, layer_scale, w_in, w_out = params
    per_piece = seed_grads.shape[0] // pieces
    pieces_in = seed_grads.reshape((pieces, per_piece) + seed_grads.shape[1:])
    returned = jnp.zeros_like(pieces_in)
    if with_weights:
        totals = (
            jnp.zeros(kernel.shape, jnp.float32),
            jnp.zeros(w_in.shape, jnp.float32),
            jnp.zeros(w_out.shape, jnp.float32),
        )
    else:
        totals = ()

    def advance(operands):
        return section_backward(operands[0], operands[1], params, with_weights)

    def pass_by(operands):
        return (operands[1], tuple((jnp.zeros_like(member) for member in totals)))

    def tick_fn(tick_idx, carry_in):
        buffer, returned_now, totals_now = carry_in
        slot_raw = tick_idx - (sections - 1 - section_idx)
        active = (slot_raw >= 0) & (slot_raw < pieces)
        slot_idx = jnp.clip(slot_raw, 0, pieces - 1)
        entry_now = tuple(
            (lax.dynamic_index_in_dim(member, slot_idx, 0, keepdims=False) for member in saved)
        )
        fed_in = jnp.where(
            section_idx == sections - 1,
            lax.dynamic_index_in_dim(pieces_in, slot_idx, 0, keepdims=False),
            buffer,
        )
        grad_in, grads_now = lax.cond(active, advance, pass_by, (entry_now, fed_in))
        totals_now = tuple((previous + fresh for previous, fresh in zip(totals_now, grads_now)))
        at_first = active & (section_idx == 0)
        returned_now = jnp.where(
            at_first,
            lax.dynamic_update_index_in_dim(returned_now, grad_in, slot_idx, 0),
            returned_now,
        )
        buffer = from_behind(grad_in, "section", -1)
        return (buffer, returned_now, totals_now)

    start_carry = (jnp.zeros_like(pieces_in[0]), returned, totals)
    unused_buffer, returned, totals = lax.fori_loop(0, pieces + sections - 1, tick_fn, start_carry)
    return (returned.reshape(seed_grads.shape), totals)


def gather_blocks(block, rows_axis):
    sections = lax.axis_size("section")
    whole = lax.all_gather(block, ("section", "dp"), axis=0, tiled=True)
    return whole.reshape((sections, -1) + whole.shape[2:])


def scatter_blocks(total):
    sections = lax.axis_size("section")
    groups = lax.axis_size("dp")
    split = total.reshape((sections * groups, total.shape[1] // groups) + total.shape[2:])
    return lax.psum_scatter(
        split.astype(jnp.bfloat16), ("section", "dp"), scatter_dimension=0, tiled=True
    ).astype(jnp.float32)


SQRT_HALF = math.sqrt(0.5)
INV_SQRT_2PI = 1.0 / math.sqrt(2.0 * math.pi)


def depthwise(inputs, kernel):
    extent = inputs.shape[1]
    padded = jnp.pad(inputs, ((0, 0), (3, 3), (3, 3), (0, 0)))
    mixture = jnp.zeros_like(inputs)
    for tap_row in range(7):
        for tap_col in range(7):
            mixture = (
                mixture
                + padded[:, tap_row : tap_row + extent, tap_col : tap_col + extent, :]
                * kernel[:, tap_row * 7 + tap_col]
            )
    return mixture


def conv_norm_back(inputs, kernel, norm_gain, scaled, inv_spread, grad_normed, with_kernel):
    grad_scaled = grad_normed * norm_gain
    first = jnp.mean(grad_scaled, axis=-1, keepdims=True)
    second = jnp.mean(grad_scaled * scaled, axis=-1, keepdims=True)
    grad_mix = inv_spread * (grad_scaled - first - scaled * second)
    grad_inputs = depthwise(grad_mix, kernel[:, ::-1])
    if not with_kernel:
        return grad_inputs, None
    extent = inputs.shape[1]
    padded = jnp.pad(inputs.astype(jnp.float32), ((0, 0), (3, 3), (3, 3), (0, 0)))
    taps = [
        jnp.sum(
            grad_mix * padded[:, tap_row : tap_row + extent, tap_col : tap_col + extent, :],
            axis=(0, 1, 2),
        )
        for tap_row in range(7)
        for tap_col in range(7)
    ]
    return grad_inputs, jnp.stack(taps, axis=-1)


def block_forward_kept(inputs, kernel, norm_gain, layer_scale, w_in, w_out):
    widened = inputs.astype(jnp.float32)
    mixture = depthwise(widened, kernel)
    centre = mixture - jnp.mean(mixture, axis=-1, keepdims=True)
    spread = jnp.mean(centre * centre, axis=-1, keepdims=True)
    inv_spread = lax.rsqrt(spread + 1e-06)
    scaled = centre * inv_spread
    normed = (scaled * norm_gain).astype(jnp.bfloat16)
    channels = inputs.shape[-1]
    up_proj = jnp.dot(normed.reshape(-1, channels), w_in, preferred_element_type=jnp.float32)
    tail = lax.erfc(-up_proj * SQRT_HALF)
    activated = (0.5 * up_proj * tail).astype(jnp.bfloat16)
    down_proj = jnp.dot(activated, w_out, preferred_element_type=jnp.float32).reshape(inputs.shape)
    result = (widened + layer_scale * down_proj).astype(jnp.bfloat16)
    return result, (inputs, normed, up_proj, tail, activated, scaled, inv_spread)


def block_backward_kept(kept, grad_out, kernel, norm_gain, layer_scale, w_in, w_out, with_weights):
    inputs, normed, up_proj, tail, activated, scaled, inv_spread = kept
    channels = inputs.shape[-1]
    outer_grad = grad_out.astype(jnp.float32)
    grad_down = (layer_scale * outer_grad).astype(jnp.bfloat16).reshape(-1, channels)
    grad_act = jnp.dot(grad_down, w_out.T, preferred_element_type=jnp.float32)
    slope_gelu = 0.5 * tail + up_proj * jnp.exp(-0.5 * up_proj * up_proj) * INV_SQRT_2PI
    grad_up = (grad_act * slope_gelu).astype(jnp.bfloat16)
    grad_normed = jnp.dot(grad_up, w_in.T, preferred_element_type=jnp.float32).reshape(inputs.shape)
    if not with_weights:
        grad_inputs, unused_kern = conv_norm_back(
            inputs, kernel, norm_gain, scaled, inv_spread, grad_normed, False
        )
        return ((outer_grad + grad_inputs).astype(jnp.bfloat16), ())
    unused_norm, norm_back = jax.vjp(conv_norm, inputs.astype(jnp.float32), kernel, norm_gain)
    grad_inputs, grad_kern, unused_gain = norm_back(grad_normed)
    grad_in = (outer_grad + grad_inputs).astype(jnp.bfloat16)
    grad_first = jnp.dot(
        normed.reshape(-1, channels).T, grad_up, preferred_element_type=jnp.float32
    )
    grad_second = jnp.dot(activated.T, grad_down, preferred_element_type=jnp.float32)
    return (grad_in, (grad_kern, grad_first, grad_second))


def network_forward(values, params):
    kernel, norm_gain, layer_scale, w_in, w_out = params
    stored = []
    for block_idx in range(kernel.shape[0]):
        values, kept = block_forward_kept(
            values, kernel[block_idx], norm_gain[block_idx], layer_scale[block_idx],
            w_in[block_idx], w_out[block_idx],
        )
        stored.append(kept)
    return values, stored


def network_backward(stored, grad_now, params, with_weights):
    kernel, norm_gain, layer_scale, w_in, w_out = params
    results = [None] * kernel.shape[0]
    for block_idx in reversed(range(kernel.shape[0])):
        grad_now, grads_now = block_backward_kept(
            stored[block_idx], grad_now, kernel[block_idx], norm_gain[block_idx],
            layer_scale[block_idx], w_in[block_idx], w_out[block_idx], with_weights,
        )
        results[block_idx] = grads_now
    return grad_now, results


def per_device_flat(features, init_noise, target, kernel, norm_gain, layer_scale, w_in, w_out):
    sections = lax.axis_size("section")
    section_idx = lax.axis_index("section")
    groups = lax.axis_size("dp")
    factor = 1.0 / math.sqrt(features.shape[0] * features.shape[1] * features.shape[2] * groups)
    own = features.shape[0] // sections

    def mine(whole):
        return lax.dynamic_slice_in_dim(whole, section_idx * own, own, 0)

    features, init_noise, target = mine(features), mine(init_noise), mine(target)
    taps = kernel.shape[-1]
    small = jnp.concatenate([kernel, norm_gain[..., None], layer_scale[..., None]], axis=-1)
    small = lax.all_gather(small, "section", axis=0, tiled=True)
    params = (
        small[..., :taps],
        small[..., taps],
        small[..., taps + 1],
        gather_blocks(w_in, 1),
        gather_blocks(w_out, 1),
    )
    clean_in = (features.astype(jnp.float32) + init_noise).astype(jnp.bfloat16)
    outputs, stored = network_forward(clean_in, params)
    seed_grads = ((outputs.astype(jnp.float32) - target.astype(jnp.float32)) * factor).astype(
        jnp.bfloat16
    )
    slope_in, unused_list = network_backward(stored, seed_grads, params, False)
    slope = slope_in.astype(jnp.float32)
    rms_value = jnp.sqrt(jnp.mean(slope * slope, axis=(1, 2, 3), keepdims=True) + 1e-06)
    delta_step = jnp.clip(init_noise + step_size * jnp.tanh(slope / rms_value), -radius, radius)
    adverse = (features.astype(jnp.float32) + delta_step).astype(jnp.bfloat16)
    outputs_adv, stored_adv = network_forward(adverse, params)
    seed_adv = ((outputs_adv.astype(jnp.float32) - target.astype(jnp.float32)) * factor).astype(
        jnp.bfloat16
    )
    unused_grad, grad_list = network_backward(stored_adv, seed_adv, params, True)
    grad_kern, grad_first, grad_second = (
        jnp.stack([grads[part_idx] for grads in grad_list]) for part_idx in range(3)
    )
    taps = grad_kern.shape[-1]
    width = grad_first.shape[-1]
    pad = (-(width + taps)) % 128
    joined = jnp.concatenate(
        [grad_first, grad_kern, jnp.zeros(grad_kern.shape[:2] + (pad,), grad_kern.dtype)], axis=-1
    )
    joined = scatter_blocks(joined)
    return (joined[..., width : width + taps], joined[..., :width], scatter_blocks(grad_second))


def per_device(features, init_noise, target, kernel, norm_gain, layer_scale, w_in, w_out):
    full_in, full_out = (
        lax.all_gather(w_in, "dp", axis=1, tiled=True),
        lax.all_gather(w_out, "dp", axis=1, tiled=True),
    )
    params = (kernel, norm_gain, layer_scale, full_in, full_out)
    pieces = MICRO // 2
    groups = lax.axis_size("dp")
    factor = 1.0 / math.sqrt(features.shape[0] * features.shape[1] * features.shape[2] * groups)
    clean_in = (features.astype(jnp.float32) + init_noise).astype(jnp.bfloat16)
    outputs, saved = run_forward(clean_in, params, pieces)
    seed_grads = ((outputs.astype(jnp.float32) - target.astype(jnp.float32)) * factor).astype(
        jnp.bfloat16
    )
    slope_in, unused_totals = run_backward(saved, seed_grads, params, pieces, False)
    slope = slope_in.astype(jnp.float32)
    rms_value = jnp.sqrt(jnp.mean(slope * slope, axis=(1, 2, 3), keepdims=True) + 1e-06)
    delta_step = jnp.clip(init_noise + step_size * jnp.tanh(slope / rms_value), -radius, radius)
    adverse = (features.astype(jnp.float32) + delta_step).astype(jnp.bfloat16)
    outputs_adv, saved_adv = run_forward(adverse, params, pieces)
    seed_adv = ((outputs_adv.astype(jnp.float32) - target.astype(jnp.float32)) * factor).astype(
        jnp.bfloat16
    )
    unused_grad, totals = run_backward(saved_adv, seed_adv, params, pieces, True)
    grad_kern, grad_first, grad_second = totals
    summed = (
        lax.psum_scatter(
            grad_kern.astype(jnp.bfloat16), "dp", scatter_dimension=1, tiled=True
        ).astype(jnp.float32),
        lax.psum_scatter(
            grad_first.astype(jnp.bfloat16), "dp", scatter_dimension=1, tiled=True
        ).astype(jnp.float32),
        lax.psum_scatter(
            grad_second.astype(jnp.bfloat16), "dp", scatter_dimension=1, tiled=True
        ).astype(jnp.float32),
    )
    return (summed[0], summed[1], summed[2])


def solution(mesh):
    def chosen(features, *rest):
        if features.shape[0] % mesh.shape["section"] == 0:
            return per_device_flat(features, *rest)
        return per_device(features, *rest)

    placed = (
        P(("group", "dp"), None, None, None),
        P(("group", "dp"), None, None, None),
        P(("group", "dp"), None, None, None),
        P("section", None, None),
        P("section", None),
        P("section", None),
        P("section", "dp", None),
        P("section", "dp", None),
    )
    return jax.shard_map(
        chosen,
        mesh=mesh,
        in_specs=placed,
        out_specs=(
            P(("group", "section"), "dp", None),
            P(("group", "section"), "dp", None),
            P(("group", "section"), "dp", None),
        ),
        check_vma=False,
    )
```

```python
import math

import jax
import jax.numpy as jnp
from jax import lax
from jax.sharding import PartitionSpec as P

MICRO = 4


radius = 0.5
step_size = 0.625


def from_behind(block, axis, distance):
    devices = range(lax.axis_size(axis))
    route = [(i - distance, i) for i in devices if i - distance in devices]
    return lax.ppermute(block, axis, route)


def conv_norm(inputs, kernel, norm_gain):
    extent = inputs.shape[1]
    padded = jnp.pad(inputs, ((0, 0), (3, 3), (3, 3), (0, 0)))
    mixture = jnp.zeros_like(inputs)
    for tap_row in range(7):
        for tap_col in range(7):
            mixture = (
                mixture
                + padded[:, tap_row : tap_row + extent, tap_col : tap_col + extent, :]
                * kernel[:, tap_row * 7 + tap_col]
            )
    centre = mixture - jnp.mean(mixture, axis=-1, keepdims=True)
    spread = jnp.mean(centre * centre, axis=-1, keepdims=True)
    return centre * lax.rsqrt(spread + 1e-06) * norm_gain


def gelu_exact(values):
    return jax.nn.gelu(values, approximate=False)


def block_forward(inputs, kernel, norm_gain, layer_scale, w_in, w_out):
    widened = inputs.astype(jnp.float32)
    normed = conv_norm(widened, kernel, norm_gain).astype(jnp.bfloat16)
    channels = inputs.shape[-1]
    up_proj = jnp.dot(normed.reshape(-1, channels), w_in, preferred_element_type=jnp.float32)
    activated = gelu_exact(up_proj).astype(jnp.bfloat16)
    down_proj = jnp.dot(activated, w_out, preferred_element_type=jnp.float32).reshape(inputs.shape)
    result = (widened + layer_scale * down_proj).astype(jnp.bfloat16)
    return (result, normed, up_proj)


def block_backward(
    inputs, normed, up_proj, grad_out, kernel, norm_gain, layer_scale, w_in, w_out, with_weights
):
    channels = inputs.shape[-1]
    outer_grad = grad_out.astype(jnp.float32)
    grad_down = (layer_scale * outer_grad).astype(jnp.bfloat16).reshape(-1, channels)
    grad_act = jnp.dot(grad_down, w_out.T, preferred_element_type=jnp.float32)
    unused_value, gelu_back = jax.vjp(gelu_exact, up_proj)
    grad_up = gelu_back(grad_act)[0].astype(jnp.bfloat16)
    grad_normed = jnp.dot(grad_up, w_in.T, preferred_element_type=jnp.float32).reshape(inputs.shape)
    unused_norm, norm_back = jax.vjp(conv_norm, inputs.astype(jnp.float32), kernel, norm_gain)
    grad_inputs, grad_kern, unused_gain = norm_back(grad_normed)
    grad_in = (outer_grad + grad_inputs).astype(jnp.bfloat16)
    if not with_weights:
        return (grad_in, ())
    activated = gelu_exact(up_proj).astype(jnp.bfloat16)
    grad_first = jnp.dot(
        normed.reshape(-1, channels).T, grad_up, preferred_element_type=jnp.float32
    )
    grad_second = jnp.dot(activated.T, grad_down, preferred_element_type=jnp.float32)
    return (grad_in, (grad_kern, grad_first, grad_second))


def section_forward(values, params):
    kernel, norm_gain, layer_scale, w_in, w_out = params
    inputs_list, normed_list, up_list = ([], [], [])
    inputs_list.append(values)
    values, normed, up_proj = block_forward(
        values, kernel[0], norm_gain[0], layer_scale[0], w_in[0], w_out[0]
    )
    normed_list.append(normed)
    up_list.append(up_proj)
    return (values, (jnp.stack(inputs_list), jnp.stack(normed_list), jnp.stack(up_list)))


def section_backward(entry_now, grad_now, params, with_weights):
    kernel, norm_gain, layer_scale, w_in, w_out = params
    inputs_all, normed_all, up_all = entry_now
    results = []
    for layer_idx in reversed(range(kernel.shape[0])):
        grad_now, grads_now = block_backward(
            inputs_all[layer_idx],
            normed_all[layer_idx],
            up_all[layer_idx],
            grad_now,
            kernel[layer_idx],
            norm_gain[layer_idx],
            layer_scale[layer_idx],
            w_in[layer_idx],
            w_out[layer_idx],
            with_weights,
        )
        results.insert(0, grads_now)
    if not with_weights:
        return (grad_now, ())
    return (
        grad_now,
        tuple((jnp.stack([member[part_idx] for member in results]) for part_idx in range(3))),
    )


def run_forward(inputs, params, pieces):
    sections = lax.axis_size("section")
    section_idx = lax.axis_index("section")
    kernel, norm_gain, layer_scale, w_in, w_out = params
    depth = kernel.shape[0]
    per_piece = inputs.shape[0] // pieces
    pieces_in = inputs.reshape((pieces, per_piece) + inputs.shape[1:])
    rows_piece = per_piece * inputs.shape[1] * inputs.shape[2]
    saved = (
        jnp.zeros((pieces, depth) + pieces_in.shape[1:], jnp.bfloat16),
        jnp.zeros((pieces, depth) + pieces_in.shape[1:], jnp.bfloat16),
        jnp.zeros((pieces, depth, rows_piece, w_in.shape[-1]), jnp.float32),
    )
    outputs = jnp.zeros_like(pieces_in)

    def advance(values):
        return section_forward(values, params)

    def pass_by(values):
        return (values, tuple((jnp.zeros(member.shape[1:], member.dtype) for member in saved)))

    def tick_fn(tick_idx, carry_in):
        buffer, saved_now, outputs_now = carry_in
        slot_raw = tick_idx - section_idx
        active = (slot_raw >= 0) & (slot_raw < pieces)
        slot_idx = jnp.clip(slot_raw, 0, pieces - 1)
        fed_in = jnp.where(
            section_idx == 0,
            lax.dynamic_index_in_dim(pieces_in, slot_idx, 0, keepdims=False),
            buffer,
        )
        result, entry_now = lax.cond(active, advance, pass_by, fed_in)
        saved_now = tuple(
            (
                jnp.where(
                    active, lax.dynamic_update_index_in_dim(previous, fresh, slot_idx, 0), previous
                )
                for previous, fresh in zip(saved_now, entry_now)
            )
        )
        at_end = active & (section_idx == sections - 1)
        outputs_now = jnp.where(
            at_end, lax.dynamic_update_index_in_dim(outputs_now, result, slot_idx, 0), outputs_now
        )
        buffer = from_behind(result, "section", 1)
        return (buffer, saved_now, outputs_now)

    start_carry = (jnp.zeros_like(pieces_in[0]), saved, outputs)
    unused_buffer, saved, outputs = lax.fori_loop(0, pieces + sections - 1, tick_fn, start_carry)
    return (outputs.reshape(inputs.shape), saved)


def run_backward(saved, seed_grads, params, pieces, with_weights):
    sections = lax.axis_size("section")
    section_idx = lax.axis_index("section")
    kernel, norm_gain, layer_scale, w_in, w_out = params
    per_piece = seed_grads.shape[0] // pieces
    pieces_in = seed_grads.reshape((pieces, per_piece) + seed_grads.shape[1:])
    returned = jnp.zeros_like(pieces_in)
    if with_weights:
        totals = (
            jnp.zeros(kernel.shape, jnp.float32),
            jnp.zeros(w_in.shape, jnp.float32),
            jnp.zeros(w_out.shape, jnp.float32),
        )
    else:
        totals = ()

    def advance(operands):
        return section_backward(operands[0], operands[1], params, with_weights)

    def pass_by(operands):
        return (operands[1], tuple((jnp.zeros_like(member) for member in totals)))

    def tick_fn(tick_idx, carry_in):
        buffer, returned_now, totals_now = carry_in
        slot_raw = tick_idx - (sections - 1 - section_idx)
        active = (slot_raw >= 0) & (slot_raw < pieces)
        slot_idx = jnp.clip(slot_raw, 0, pieces - 1)
        entry_now = tuple(
            (lax.dynamic_index_in_dim(member, slot_idx, 0, keepdims=False) for member in saved)
        )
        fed_in = jnp.where(
            section_idx == sections - 1,
            lax.dynamic_index_in_dim(pieces_in, slot_idx, 0, keepdims=False),
            buffer,
        )
        grad_in, grads_now = lax.cond(active, advance, pass_by, (entry_now, fed_in))
        totals_now = tuple((previous + fresh for previous, fresh in zip(totals_now, grads_now)))
        at_first = active & (section_idx == 0)
        returned_now = jnp.where(
            at_first,
            lax.dynamic_update_index_in_dim(returned_now, grad_in, slot_idx, 0),
            returned_now,
        )
        buffer = from_behind(grad_in, "section", -1)
        return (buffer, returned_now, totals_now)

    start_carry = (jnp.zeros_like(pieces_in[0]), returned, totals)
    unused_buffer, returned, totals = lax.fori_loop(0, pieces + sections - 1, tick_fn, start_carry)
    return (returned.reshape(seed_grads.shape), totals)


def gather_blocks(block, rows_axis):
    sections = lax.axis_size("section")
    whole = lax.all_gather(block, ("section", "dp"), axis=0, tiled=True)
    return whole.reshape((sections, -1) + whole.shape[2:])


def scatter_blocks(total, widen=True):
    sections = lax.axis_size("section")
    groups = lax.axis_size("dp")
    split = total.reshape((sections * groups, total.shape[1] // groups) + total.shape[2:])
    summed = lax.psum_scatter(
        split.astype(jnp.bfloat16), ("section", "dp"), scatter_dimension=0, tiled=True
    )
    return summed.astype(jnp.float32) if widen else summed


SQRT_HALF = math.sqrt(0.5)
INV_SQRT_2PI = 1.0 / math.sqrt(2.0 * math.pi)


def block_forward_kept(inputs, kernel, norm_gain, layer_scale, w_in, w_out):
    widened = inputs.astype(jnp.float32)
    normed = conv_norm(widened, kernel, norm_gain).astype(jnp.bfloat16)
    channels = inputs.shape[-1]
    up_proj = jnp.dot(normed.reshape(-1, channels), w_in, preferred_element_type=jnp.float32)
    tail = lax.erfc(-up_proj * SQRT_HALF)
    activated = (0.5 * up_proj * tail).astype(jnp.bfloat16)
    down_proj = jnp.dot(activated, w_out, preferred_element_type=jnp.float32).reshape(inputs.shape)
    result = (widened + layer_scale * down_proj).astype(jnp.bfloat16)
    return result, (inputs, normed, up_proj, tail, activated)


def block_backward_kept(kept, grad_out, kernel, norm_gain, layer_scale, w_in, w_out, with_weights):
    inputs, normed, up_proj, tail, activated = kept
    channels = inputs.shape[-1]
    outer_grad = grad_out.astype(jnp.float32)
    grad_down = (layer_scale * outer_grad).astype(jnp.bfloat16).reshape(-1, channels)
    grad_act = jnp.dot(grad_down, w_out.T, preferred_element_type=jnp.float32)
    slope_gelu = 0.5 * tail + up_proj * jnp.exp(-0.5 * up_proj * up_proj) * INV_SQRT_2PI
    grad_up = (grad_act * slope_gelu).astype(jnp.bfloat16)
    grad_normed = jnp.dot(grad_up, w_in.T, preferred_element_type=jnp.float32).reshape(inputs.shape)
    unused_norm, norm_back = jax.vjp(conv_norm, inputs.astype(jnp.float32), kernel, norm_gain)
    grad_inputs, grad_kern, unused_gain = norm_back(grad_normed)
    grad_in = (outer_grad + grad_inputs).astype(jnp.bfloat16)
    if not with_weights:
        return (grad_in, ())
    grad_first = jnp.dot(
        normed.reshape(-1, channels).T, grad_up, preferred_element_type=jnp.float32
    )
    grad_second = jnp.dot(activated.T, grad_down, preferred_element_type=jnp.float32)
    return (grad_in, (grad_kern, grad_first, grad_second))


def network_forward(values, params):
    kernel, norm_gain, layer_scale, w_in, w_out = params
    stored = []
    for block_idx in range(kernel.shape[0]):
        values, kept = block_forward_kept(
            values, kernel[block_idx], norm_gain[block_idx], layer_scale[block_idx],
            w_in[block_idx], w_out[block_idx],
        )
        stored.append(kept)
    return values, stored


def network_backward(stored, grad_now, params, with_weights):
    kernel, norm_gain, layer_scale, w_in, w_out = params
    results = [None] * kernel.shape[0]
    for block_idx in reversed(range(kernel.shape[0])):
        grad_now, grads_now = block_backward_kept(
            stored[block_idx], grad_now, kernel[block_idx], norm_gain[block_idx],
            layer_scale[block_idx], w_in[block_idx], w_out[block_idx], with_weights,
        )
        results[block_idx] = grads_now
    return grad_now, results


def per_device_flat(features, init_noise, target, kernel, norm_gain, layer_scale, w_in, w_out):
    sections = lax.axis_size("section")
    section_idx = lax.axis_index("section")
    groups = lax.axis_size("dp")
    factor = 1.0 / math.sqrt(features.shape[0] * features.shape[1] * features.shape[2] * groups)
    own = features.shape[0] // sections

    def mine(whole):
        return lax.dynamic_slice_in_dim(whole, section_idx * own, own, 0)

    features, init_noise, target = mine(features), mine(init_noise), mine(target)
    taps = kernel.shape[-1]
    small = jnp.concatenate([kernel, norm_gain[..., None], layer_scale[..., None]], axis=-1)
    small = lax.all_gather(small, "section", axis=0, tiled=True)
    params = (
        small[..., :taps],
        small[..., taps],
        small[..., taps + 1],
        gather_blocks(w_in, 1),
        gather_blocks(w_out, 1),
    )
    clean_in = (features.astype(jnp.float32) + init_noise).astype(jnp.bfloat16)
    outputs, stored = network_forward(clean_in, params)
    seed_grads = ((outputs.astype(jnp.float32) - target.astype(jnp.float32)) * factor).astype(
        jnp.bfloat16
    )
    slope_in, unused_list = network_backward(stored, seed_grads, params, False)
    slope = slope_in.astype(jnp.float32)
    rms_value = jnp.sqrt(jnp.mean(slope * slope, axis=(1, 2, 3), keepdims=True) + 1e-06)
    delta_step = jnp.clip(init_noise + step_size * jnp.tanh(slope / rms_value), -radius, radius)
    adverse = (features.astype(jnp.float32) + delta_step).astype(jnp.bfloat16)
    outputs_adv, stored_adv = network_forward(adverse, params)
    seed_adv = ((outputs_adv.astype(jnp.float32) - target.astype(jnp.float32)) * factor).astype(
        jnp.bfloat16
    )
    unused_grad, grad_list = network_backward(stored_adv, seed_adv, params, True)
    grad_kern, grad_first, grad_second = (
        jnp.stack([grads[part_idx] for grads in grad_list]) for part_idx in range(3)
    )
    taps = grad_kern.shape[-1]
    width = grad_first.shape[-1]
    pad = (-(width + taps)) % 128
    joined = jnp.concatenate(
        [grad_first, grad_kern, jnp.zeros(grad_kern.shape[:2] + (pad,), grad_kern.dtype)], axis=-1
    )
    joined = scatter_blocks(joined, False)
    return (
        joined[..., width : width + taps].astype(jnp.float32),
        joined[..., :width].astype(jnp.float32),
        scatter_blocks(grad_second),
    )


def per_device(features, init_noise, target, kernel, norm_gain, layer_scale, w_in, w_out):
    full_in, full_out = (
        lax.all_gather(w_in, "dp", axis=1, tiled=True),
        lax.all_gather(w_out, "dp", axis=1, tiled=True),
    )
    params = (kernel, norm_gain, layer_scale, full_in, full_out)
    pieces = MICRO // 2
    groups = lax.axis_size("dp")
    factor = 1.0 / math.sqrt(features.shape[0] * features.shape[1] * features.shape[2] * groups)
    clean_in = (features.astype(jnp.float32) + init_noise).astype(jnp.bfloat16)
    outputs, saved = run_forward(clean_in, params, pieces)
    seed_grads = ((outputs.astype(jnp.float32) - target.astype(jnp.float32)) * factor).astype(
        jnp.bfloat16
    )
    slope_in, unused_totals = run_backward(saved, seed_grads, params, pieces, False)
    slope = slope_in.astype(jnp.float32)
    rms_value = jnp.sqrt(jnp.mean(slope * slope, axis=(1, 2, 3), keepdims=True) + 1e-06)
    delta_step = jnp.clip(init_noise + step_size * jnp.tanh(slope / rms_value), -radius, radius)
    adverse = (features.astype(jnp.float32) + delta_step).astype(jnp.bfloat16)
    outputs_adv, saved_adv = run_forward(adverse, params, pieces)
    seed_adv = ((outputs_adv.astype(jnp.float32) - target.astype(jnp.float32)) * factor).astype(
        jnp.bfloat16
    )
    unused_grad, totals = run_backward(saved_adv, seed_adv, params, pieces, True)
    grad_kern, grad_first, grad_second = totals
    summed = (
        lax.psum_scatter(
            grad_kern.astype(jnp.bfloat16), "dp", scatter_dimension=1, tiled=True
        ).astype(jnp.float32),
        lax.psum_scatter(
            grad_first.astype(jnp.bfloat16), "dp", scatter_dimension=1, tiled=True
        ).astype(jnp.float32),
        lax.psum_scatter(
            grad_second.astype(jnp.bfloat16), "dp", scatter_dimension=1, tiled=True
        ).astype(jnp.float32),
    )
    return (summed[0], summed[1], summed[2])


def solution(mesh):
    def chosen(features, *rest):
        if features.shape[0] % mesh.shape["section"] == 0:
            return per_device_flat(features, *rest)
        return per_device(features, *rest)

    placed = (
        P(("group", "dp"), None, None, None),
        P(("group", "dp"), None, None, None),
        P(("group", "dp"), None, None, None),
        P("section", None, None),
        P("section", None),
        P("section", None),
        P("section", "dp", None),
        P("section", "dp", None),
    )
    return jax.shard_map(
        chosen,
        mesh=mesh,
        in_specs=placed,
        out_specs=(
            P(("group", "section"), "dp", None),
            P(("group", "section"), "dp", None),
            P(("group", "section"), "dp", None),
        ),
        check_vma=False,
    )
```

```python
import math

import jax
import jax.numpy as jnp
from jax import lax
from jax.sharding import PartitionSpec as P

MICRO = 4


radius = 0.5
step_size = 0.625


def from_behind(block, axis, distance):
    devices = range(lax.axis_size(axis))
    route = [(i - distance, i) for i in devices if i - distance in devices]
    return lax.ppermute(block, axis, route)


def conv_norm(inputs, kernel, norm_gain):
    extent = inputs.shape[1]
    padded = jnp.pad(inputs, ((0, 0), (3, 3), (3, 3), (0, 0)))
    mixture = jnp.zeros_like(inputs)
    for tap_row in range(7):
        for tap_col in range(7):
            mixture = (
                mixture
                + padded[:, tap_row : tap_row + extent, tap_col : tap_col + extent, :]
                * kernel[:, tap_row * 7 + tap_col]
            )
    centre = mixture - jnp.mean(mixture, axis=-1, keepdims=True)
    spread = jnp.mean(centre * centre, axis=-1, keepdims=True)
    return centre * lax.rsqrt(spread + 1e-06) * norm_gain


def gelu_exact(values):
    return jax.nn.gelu(values, approximate=False)


def block_forward(inputs, kernel, norm_gain, layer_scale, w_in, w_out):
    widened = inputs.astype(jnp.float32)
    normed = conv_norm(widened, kernel, norm_gain).astype(jnp.bfloat16)
    channels = inputs.shape[-1]
    up_proj = jnp.dot(normed.reshape(-1, channels), w_in, preferred_element_type=jnp.float32)
    activated = gelu_exact(up_proj).astype(jnp.bfloat16)
    down_proj = jnp.dot(activated, w_out, preferred_element_type=jnp.float32).reshape(inputs.shape)
    result = (widened + layer_scale * down_proj).astype(jnp.bfloat16)
    return (result, normed, up_proj)


def block_backward(
    inputs, normed, up_proj, grad_out, kernel, norm_gain, layer_scale, w_in, w_out, with_weights
):
    channels = inputs.shape[-1]
    outer_grad = grad_out.astype(jnp.float32)
    grad_down = (layer_scale * outer_grad).astype(jnp.bfloat16).reshape(-1, channels)
    grad_act = jnp.dot(grad_down, w_out.T, preferred_element_type=jnp.float32)
    unused_value, gelu_back = jax.vjp(gelu_exact, up_proj)
    grad_up = gelu_back(grad_act)[0].astype(jnp.bfloat16)
    grad_normed = jnp.dot(grad_up, w_in.T, preferred_element_type=jnp.float32).reshape(inputs.shape)
    unused_norm, norm_back = jax.vjp(conv_norm, inputs.astype(jnp.float32), kernel, norm_gain)
    grad_inputs, grad_kern, unused_gain = norm_back(grad_normed)
    grad_in = (outer_grad + grad_inputs).astype(jnp.bfloat16)
    if not with_weights:
        return (grad_in, ())
    activated = gelu_exact(up_proj).astype(jnp.bfloat16)
    grad_first = jnp.dot(
        normed.reshape(-1, channels).T, grad_up, preferred_element_type=jnp.float32
    )
    grad_second = jnp.dot(activated.T, grad_down, preferred_element_type=jnp.float32)
    return (grad_in, (grad_kern, grad_first, grad_second))


def section_forward(values, params):
    kernel, norm_gain, layer_scale, w_in, w_out = params
    inputs_list, normed_list, up_list = ([], [], [])
    inputs_list.append(values)
    values, normed, up_proj = block_forward(
        values, kernel[0], norm_gain[0], layer_scale[0], w_in[0], w_out[0]
    )
    normed_list.append(normed)
    up_list.append(up_proj)
    return (values, (jnp.stack(inputs_list), jnp.stack(normed_list), jnp.stack(up_list)))


def section_backward(entry_now, grad_now, params, with_weights):
    kernel, norm_gain, layer_scale, w_in, w_out = params
    inputs_all, normed_all, up_all = entry_now
    results = []
    for layer_idx in reversed(range(kernel.shape[0])):
        grad_now, grads_now = block_backward(
            inputs_all[layer_idx],
            normed_all[layer_idx],
            up_all[layer_idx],
            grad_now,
            kernel[layer_idx],
            norm_gain[layer_idx],
            layer_scale[layer_idx],
            w_in[layer_idx],
            w_out[layer_idx],
            with_weights,
        )
        results.insert(0, grads_now)
    if not with_weights:
        return (grad_now, ())
    return (
        grad_now,
        tuple((jnp.stack([member[part_idx] for member in results]) for part_idx in range(3))),
    )


def run_forward(inputs, params, pieces):
    sections = lax.axis_size("section")
    section_idx = lax.axis_index("section")
    kernel, norm_gain, layer_scale, w_in, w_out = params
    depth = kernel.shape[0]
    per_piece = inputs.shape[0] // pieces
    pieces_in = inputs.reshape((pieces, per_piece) + inputs.shape[1:])
    rows_piece = per_piece * inputs.shape[1] * inputs.shape[2]
    saved = (
        jnp.zeros((pieces, depth) + pieces_in.shape[1:], jnp.bfloat16),
        jnp.zeros((pieces, depth) + pieces_in.shape[1:], jnp.bfloat16),
        jnp.zeros((pieces, depth, rows_piece, w_in.shape[-1]), jnp.float32),
    )
    outputs = jnp.zeros_like(pieces_in)

    def advance(values):
        return section_forward(values, params)

    def pass_by(values):
        return (values, tuple((jnp.zeros(member.shape[1:], member.dtype) for member in saved)))

    def tick_fn(tick_idx, carry_in):
        buffer, saved_now, outputs_now = carry_in
        slot_raw = tick_idx - section_idx
        active = (slot_raw >= 0) & (slot_raw < pieces)
        slot_idx = jnp.clip(slot_raw, 0, pieces - 1)
        fed_in = jnp.where(
            section_idx == 0,
            lax.dynamic_index_in_dim(pieces_in, slot_idx, 0, keepdims=False),
            buffer,
        )
        result, entry_now = lax.cond(active, advance, pass_by, fed_in)
        saved_now = tuple(
            (
                jnp.where(
                    active, lax.dynamic_update_index_in_dim(previous, fresh, slot_idx, 0), previous
                )
                for previous, fresh in zip(saved_now, entry_now)
            )
        )
        at_end = active & (section_idx == sections - 1)
        outputs_now = jnp.where(
            at_end, lax.dynamic_update_index_in_dim(outputs_now, result, slot_idx, 0), outputs_now
        )
        buffer = from_behind(result, "section", 1)
        return (buffer, saved_now, outputs_now)

    start_carry = (jnp.zeros_like(pieces_in[0]), saved, outputs)
    unused_buffer, saved, outputs = lax.fori_loop(0, pieces + sections - 1, tick_fn, start_carry)
    return (outputs.reshape(inputs.shape), saved)


def run_backward(saved, seed_grads, params, pieces, with_weights):
    sections = lax.axis_size("section")
    section_idx = lax.axis_index("section")
    kernel, norm_gain, layer_scale, w_in, w_out = params
    per_piece = seed_grads.shape[0] // pieces
    pieces_in = seed_grads.reshape((pieces, per_piece) + seed_grads.shape[1:])
    returned = jnp.zeros_like(pieces_in)
    if with_weights:
        totals = (
            jnp.zeros(kernel.shape, jnp.float32),
            jnp.zeros(w_in.shape, jnp.float32),
            jnp.zeros(w_out.shape, jnp.float32),
        )
    else:
        totals = ()

    def advance(operands):
        return section_backward(operands[0], operands[1], params, with_weights)

    def pass_by(operands):
        return (operands[1], tuple((jnp.zeros_like(member) for member in totals)))

    def tick_fn(tick_idx, carry_in):
        buffer, returned_now, totals_now = carry_in
        slot_raw = tick_idx - (sections - 1 - section_idx)
        active = (slot_raw >= 0) & (slot_raw < pieces)
        slot_idx = jnp.clip(slot_raw, 0, pieces - 1)
        entry_now = tuple(
            (lax.dynamic_index_in_dim(member, slot_idx, 0, keepdims=False) for member in saved)
        )
        fed_in = jnp.where(
            section_idx == sections - 1,
            lax.dynamic_index_in_dim(pieces_in, slot_idx, 0, keepdims=False),
            buffer,
        )
        grad_in, grads_now = lax.cond(active, advance, pass_by, (entry_now, fed_in))
        totals_now = tuple((previous + fresh for previous, fresh in zip(totals_now, grads_now)))
        at_first = active & (section_idx == 0)
        returned_now = jnp.where(
            at_first,
            lax.dynamic_update_index_in_dim(returned_now, grad_in, slot_idx, 0),
            returned_now,
        )
        buffer = from_behind(grad_in, "section", -1)
        return (buffer, returned_now, totals_now)

    start_carry = (jnp.zeros_like(pieces_in[0]), returned, totals)
    unused_buffer, returned, totals = lax.fori_loop(0, pieces + sections - 1, tick_fn, start_carry)
    return (returned.reshape(seed_grads.shape), totals)


def gather_blocks(block, rows_axis):
    sections = lax.axis_size("section")
    whole = lax.all_gather(block, ("section", "dp"), axis=0, tiled=True)
    return whole.reshape((sections, -1) + whole.shape[2:])


def scatter_blocks(total):
    sections = lax.axis_size("section")
    groups = lax.axis_size("dp")
    split = total.reshape((sections * groups, total.shape[1] // groups) + total.shape[2:])
    return lax.psum_scatter(
        split.astype(jnp.bfloat16), ("section", "dp"), scatter_dimension=0, tiled=True
    ).astype(jnp.float32)


SQRT_HALF = math.sqrt(0.5)
INV_SQRT_2PI = 1.0 / math.sqrt(2.0 * math.pi)


def depthwise(inputs, kernel):
    extent = inputs.shape[1]
    padded = jnp.pad(inputs, ((0, 0), (3, 3), (3, 3), (0, 0)))
    mixture = jnp.zeros_like(inputs)
    for tap_row in range(7):
        for tap_col in range(7):
            mixture = (
                mixture
                + padded[:, tap_row : tap_row + extent, tap_col : tap_col + extent, :]
                * kernel[:, tap_row * 7 + tap_col]
            )
    return mixture


def conv_norm_back(inputs, kernel, norm_gain, scaled, inv_spread, grad_normed, with_kernel):
    grad_scaled = grad_normed * norm_gain
    first = jnp.mean(grad_scaled, axis=-1, keepdims=True)
    second = jnp.mean(grad_scaled * scaled, axis=-1, keepdims=True)
    grad_mix = inv_spread * (grad_scaled - first - scaled * second)
    grad_inputs = depthwise(grad_mix, kernel[:, ::-1])
    if not with_kernel:
        return grad_inputs, None
    extent = inputs.shape[1]
    padded = jnp.pad(inputs.astype(jnp.float32), ((0, 0), (3, 3), (3, 3), (0, 0)))
    taps = [
        jnp.sum(
            grad_mix * padded[:, tap_row : tap_row + extent, tap_col : tap_col + extent, :],
            axis=(0, 1, 2),
        )
        for tap_row in range(7)
        for tap_col in range(7)
    ]
    return grad_inputs, jnp.stack(taps, axis=-1)


def block_forward_kept(inputs, kernel, norm_gain, layer_scale, w_in, w_out):
    widened = inputs.astype(jnp.float32)
    normed = conv_norm(widened, kernel, norm_gain).astype(jnp.bfloat16)
    channels = inputs.shape[-1]
    up_proj = jnp.dot(normed.reshape(-1, channels), w_in, preferred_element_type=jnp.float32)
    tail = lax.erfc(-up_proj * SQRT_HALF)
    activated = (0.5 * up_proj * tail).astype(jnp.bfloat16)
    down_proj = jnp.dot(activated, w_out, preferred_element_type=jnp.float32).reshape(inputs.shape)
    result = (widened + layer_scale * down_proj).astype(jnp.bfloat16)
    return result, (inputs, normed, up_proj, tail, activated)


def block_backward_kept(kept, grad_out, kernel, norm_gain, layer_scale, w_in, w_out, with_weights):
    inputs, normed, up_proj, tail, activated = kept
    channels = inputs.shape[-1]
    outer_grad = grad_out.astype(jnp.float32)
    grad_down = (layer_scale * outer_grad).astype(jnp.bfloat16).reshape(-1, channels)
    grad_act = jnp.dot(grad_down, w_out.T, preferred_element_type=jnp.float32)
    slope_gelu = 0.5 * tail + up_proj * jnp.exp(-0.5 * up_proj * up_proj) * INV_SQRT_2PI
    grad_up = (grad_act * slope_gelu).astype(jnp.bfloat16)
    grad_normed = jnp.dot(grad_up, w_in.T, preferred_element_type=jnp.float32).reshape(inputs.shape)
    if not with_weights:
        mixture = depthwise(inputs.astype(jnp.float32), kernel)
        centre = mixture - jnp.mean(mixture, axis=-1, keepdims=True)
        inv_spread = lax.rsqrt(jnp.mean(centre * centre, axis=-1, keepdims=True) + 1e-06)
        grad_inputs, unused_kern = conv_norm_back(
            inputs, kernel, norm_gain, centre * inv_spread, inv_spread, grad_normed, False
        )
        return ((outer_grad + grad_inputs).astype(jnp.bfloat16), ())
    unused_norm, norm_back = jax.vjp(conv_norm, inputs.astype(jnp.float32), kernel, norm_gain)
    grad_inputs, grad_kern, unused_gain = norm_back(grad_normed)
    grad_in = (outer_grad + grad_inputs).astype(jnp.bfloat16)
    grad_first = jnp.dot(
        normed.reshape(-1, channels).T, grad_up, preferred_element_type=jnp.float32
    )
    grad_second = jnp.dot(activated.T, grad_down, preferred_element_type=jnp.float32)
    return (grad_in, (grad_kern, grad_first, grad_second))


def network_forward(values, params):
    kernel, norm_gain, layer_scale, w_in, w_out = params
    stored = []
    for block_idx in range(kernel.shape[0]):
        values, kept = block_forward_kept(
            values, kernel[block_idx], norm_gain[block_idx], layer_scale[block_idx],
            w_in[block_idx], w_out[block_idx],
        )
        stored.append(kept)
    return values, stored


def network_backward(stored, grad_now, params, with_weights):
    kernel, norm_gain, layer_scale, w_in, w_out = params
    results = [None] * kernel.shape[0]
    for block_idx in reversed(range(kernel.shape[0])):
        grad_now, grads_now = block_backward_kept(
            stored[block_idx], grad_now, kernel[block_idx], norm_gain[block_idx],
            layer_scale[block_idx], w_in[block_idx], w_out[block_idx], with_weights,
        )
        results[block_idx] = grads_now
    return grad_now, results


def per_device_flat(features, init_noise, target, kernel, norm_gain, layer_scale, w_in, w_out):
    sections = lax.axis_size("section")
    section_idx = lax.axis_index("section")
    groups = lax.axis_size("dp")
    factor = 1.0 / math.sqrt(features.shape[0] * features.shape[1] * features.shape[2] * groups)
    own = features.shape[0] // sections

    def mine(whole):
        return lax.dynamic_slice_in_dim(whole, section_idx * own, own, 0)

    features, init_noise, target = mine(features), mine(init_noise), mine(target)
    taps = kernel.shape[-1]
    small = jnp.concatenate([kernel, norm_gain[..., None], layer_scale[..., None]], axis=-1)
    small = lax.all_gather(small, "section", axis=0, tiled=True)
    params = (
        small[..., :taps],
        small[..., taps],
        small[..., taps + 1],
        gather_blocks(w_in, 1),
        gather_blocks(w_out, 1),
    )
    clean_in = (features.astype(jnp.float32) + init_noise).astype(jnp.bfloat16)
    outputs, stored = network_forward(clean_in, params)
    seed_grads = ((outputs.astype(jnp.float32) - target.astype(jnp.float32)) * factor).astype(
        jnp.bfloat16
    )
    slope_in, unused_list = network_backward(stored, seed_grads, params, False)
    slope = slope_in.astype(jnp.float32)
    rms_value = jnp.sqrt(jnp.mean(slope * slope, axis=(1, 2, 3), keepdims=True) + 1e-06)
    delta_step = jnp.clip(init_noise + step_size * jnp.tanh(slope / rms_value), -radius, radius)
    adverse = (features.astype(jnp.float32) + delta_step).astype(jnp.bfloat16)
    outputs_adv, stored_adv = network_forward(adverse, params)
    seed_adv = ((outputs_adv.astype(jnp.float32) - target.astype(jnp.float32)) * factor).astype(
        jnp.bfloat16
    )
    unused_grad, grad_list = network_backward(stored_adv, seed_adv, params, True)
    grad_kern, grad_first, grad_second = (
        jnp.stack([grads[part_idx] for grads in grad_list]) for part_idx in range(3)
    )
    taps = grad_kern.shape[-1]
    width = grad_first.shape[-1]
    pad = (-(width + taps)) % 128
    joined = jnp.concatenate(
        [grad_first, grad_kern, jnp.zeros(grad_kern.shape[:2] + (pad,), grad_kern.dtype)], axis=-1
    )
    joined = scatter_blocks(joined)
    return (joined[..., width : width + taps], joined[..., :width], scatter_blocks(grad_second))


def per_device(features, init_noise, target, kernel, norm_gain, layer_scale, w_in, w_out):
    full_in, full_out = (
        lax.all_gather(w_in, "dp", axis=1, tiled=True),
        lax.all_gather(w_out, "dp", axis=1, tiled=True),
    )
    params = (kernel, norm_gain, layer_scale, full_in, full_out)
    pieces = MICRO // 2
    groups = lax.axis_size("dp")
    factor = 1.0 / math.sqrt(features.shape[0] * features.shape[1] * features.shape[2] * groups)
    clean_in = (features.astype(jnp.float32) + init_noise).astype(jnp.bfloat16)
    outputs, saved = run_forward(clean_in, params, pieces)
    seed_grads = ((outputs.astype(jnp.float32) - target.astype(jnp.float32)) * factor).astype(
        jnp.bfloat16
    )
    slope_in, unused_totals = run_backward(saved, seed_grads, params, pieces, False)
    slope = slope_in.astype(jnp.float32)
    rms_value = jnp.sqrt(jnp.mean(slope * slope, axis=(1, 2, 3), keepdims=True) + 1e-06)
    delta_step = jnp.clip(init_noise + step_size * jnp.tanh(slope / rms_value), -radius, radius)
    adverse = (features.astype(jnp.float32) + delta_step).astype(jnp.bfloat16)
    outputs_adv, saved_adv = run_forward(adverse, params, pieces)
    seed_adv = ((outputs_adv.astype(jnp.float32) - target.astype(jnp.float32)) * factor).astype(
        jnp.bfloat16
    )
    unused_grad, totals = run_backward(saved_adv, seed_adv, params, pieces, True)
    grad_kern, grad_first, grad_second = totals
    summed = (
        lax.psum_scatter(
            grad_kern.astype(jnp.bfloat16), "dp", scatter_dimension=1, tiled=True
        ).astype(jnp.float32),
        lax.psum_scatter(
            grad_first.astype(jnp.bfloat16), "dp", scatter_dimension=1, tiled=True
        ).astype(jnp.float32),
        lax.psum_scatter(
            grad_second.astype(jnp.bfloat16), "dp", scatter_dimension=1, tiled=True
        ).astype(jnp.float32),
    )
    return (summed[0], summed[1], summed[2])


def solution(mesh):
    def chosen(features, *rest):
        if features.shape[0] % mesh.shape["section"] == 0:
            return per_device_flat(features, *rest)
        return per_device(features, *rest)

    placed = (
        P(("group", "dp"), None, None, None),
        P(("group", "dp"), None, None, None),
        P(("group", "dp"), None, None, None),
        P("section", None, None),
        P("section", None),
        P("section", None),
        P("section", "dp", None),
        P("section", "dp", None),
    )
    return jax.shard_map(
        chosen,
        mesh=mesh,
        in_specs=placed,
        out_specs=(
            P(("group", "section"), "dp", None),
            P(("group", "section"), "dp", None),
            P(("group", "section"), "dp", None),
        ),
        check_vma=False,
    )
```
